128 devices in a mesh: leaf: 4 (over x), blk: 32 (over y, z, core).
Axes of the slice: x: 4, y: 4, z: 4, core: 2. Of those that a mesh axis runs over, the one named last changes fastest.
Arguments:
- diag_blocks: float32 [4, 512, 512], P('leaf'), as said below
- panel: float32 [4, 128, 256, 512], P('leaf', 'blk'), may hold values from -1.2 to 1.2
- local_targets: bfloat16 [4, 2560, 256, 256], P('leaf', 'blk'), may hold values from -6 to 6
- local_pairs: int32 [4, 2560, 2], P('leaf', 'blk'), may hold values from -1 to 127, as said below
- top_targets: bfloat16 [32, 16, 256, 256], P('blk', 'leaf'), may hold values from -6 to 6
- top_pairs: int32 [32, 16, 2], P('blk'), may hold values from 0 to 255
- top_pattern: int32 [4, 256], P('leaf'), may hold values from -1 to 127, as said below
Outputs:
- panel_factor: bfloat16 [4, 128, 256, 512], P('leaf', 'blk')
- local_updated: bfloat16 [4, 2560, 256, 256], P('leaf', 'blk')
- top_updated: bfloat16 [32, 16, 256, 256], P('blk', 'leaf')
The draws below stay inside these ranges and needn't reach their ends.
Inputs may be any that keep to these rules, and one draw needn't show every extreme that they name: Each diag_blocks[g] is symmetric positive definite with smallest eigenvalue 0.5 or more. `local_pairs`: empty slots hold -1 in both columns; on each device the live slots come first; some device has all 80 slots live. `top_pattern`: in each group every panel row 0 to 127 stands at exactly one ancestor row; the other ancestor rows hold -1.
All inputs are finite; a program needn't handle non-finite values.
Results may differ from the reference program's by a relative error of at most 0.014.
Values may be sent and summed in bfloat16 or wider, within the bound.
No kernel may reach another device: no remote copies, remote signals or barrier semaphores. Data moves between devices by JAX's collectives and lax.ppermute only.
A program may use at most 192 MiB of HBM per device.

```python
import jax
import jax.numpy as jnp
from jax import lax

B = 256
TOP_DEV = 4
TL_DEV = 80
RG = 128
NA = 256
N_LEAF = 4
N_BLK = 32


def draw_diag_blocks(key, part):
    order_size = 2 * B
    base = jax.random.normal(key, (N_LEAF, order_size, order_size), jnp.float32)
    gram = jnp.einsum('gik,gjk->gij', base, base, precision=lax.Precision.HIGHEST) / order_size
    return gram + 0.5 * jnp.eye(order_size, dtype=jnp.float32)[None]


def draw_local_pairs(key, part):
    total = N_LEAF * N_BLK
    key_draws, key_full, key_rows = jax.random.split(key, 3)
    draws = jax.random.randint(key_draws, (total,), 1, TL_DEV + 1)
    counts = jnp.maximum(draws * draws // TL_DEV, 1)
    fullest = jax.random.randint(key_full, (), 0, total)
    counts = jnp.where(jnp.arange(total) == fullest, TL_DEV, counts)
    chosen = jax.random.randint(key_rows, (total, TL_DEV, 2), 0, RG)
    live = jnp.arange(TL_DEV)[None, :] < counts[:, None]
    pairs = jnp.where(live[:, :, None], chosen, -1)
    return pairs.reshape(N_LEAF, N_BLK * TL_DEV, 2).astype(jnp.int32)


def draw_top_pattern(key, part):
    group_keys = jax.random.split(key, N_LEAF)

    def one_group(group_key):
        ordering = jax.random.permutation(group_key, NA)
        ranking = jnp.argsort(ordering)
        return jnp.where(ranking < RG, ranking, -1)
    return jax.vmap(one_group)(group_keys).astype(jnp.int32)


def with_ends(result, key, least, top_value):
    longest = result.shape.index(max(result.shape))
    spots = []
    for shift in (0, 1):
        where = [jax.random.randint(jax.random.fold_in(key, axis), (), 0, length) for axis, length in enumerate(result.shape)]
        where[longest] = (where[longest] + shift) % result.shape[longest]
        spots.append(tuple(where))
    return result.at[spots[0]].set(least).at[spots[1]].set(top_value)


def levels(stream_key, extent, shards, least, top_value):
    gain, own = 1.0, jax.random.fold_in(stream_key, 6)
    for position, parts in shards:
        steps = jnp.exp(jax.random.uniform(jax.random.fold_in(own, position), (parts,), jnp.float32, least / len(shards), top_value / len(shards)))
        gain = gain * jnp.repeat(steps, extent[position] // parts).reshape([-1 if axis == position else 1 for axis in range(len(extent))])
    return gain


def scatter_about(own_key, extent, deviation, reach, cuts=(), kind=jnp.bfloat16):
    entries = jax.random.normal(own_key, extent, jnp.float32) * deviation
    if len(cuts) > 0:
        entries = levels(own_key, extent, cuts, -0.22, 0.18) * entries
    return jnp.clip(entries, min=-reach, max=reach).astype(kind)


def setup_inputs(seed: int = 0) -> dict:
    splits = jax.random.split(jax.random.key(seed), 8)
    diag_blocks = draw_diag_blocks(jax.random.fold_in(splits[7], 71), 0)
    panel = scatter_about(splits[1], (N_LEAF, RG, B, 2 * B), 0.2, 1.2, ((0, 4), (1, 32)), jnp.float32)
    local_targets = scatter_about(splits[2], (N_LEAF, N_BLK * TL_DEV, B, B), 1.0, 6.0, ((0, 4), (1, 32)))
    local_pairs = draw_local_pairs(jax.random.fold_in(splits[7], 71), 0)
    top_targets = scatter_about(splits[4], (N_BLK, N_LEAF * TOP_DEV, B, B), 1.0, 6.0, ((0, 32), (1, 4)))
    top_pairs = with_ends(jax.random.randint(splits[5], (N_BLK, N_LEAF * TOP_DEV, 2), 0, NA), jax.random.fold_in(splits[5], 1), 0, NA - 1).astype(jnp.int32)
    top_pattern = draw_top_pattern(jax.random.fold_in(splits[7], 71), 0)
    return dict(diag_blocks=diag_blocks, panel=panel, local_targets=local_targets, local_pairs=local_pairs, top_targets=top_targets, top_pairs=top_pairs, top_pattern=top_pattern)


def factor_group(diagonal, rows):
    width = diagonal.shape[0] // 2
    count = rows.shape[0]
    factor_full = jnp.linalg.cholesky(diagonal)
    upper_left = factor_full[:width, :width]
    lower_left = factor_full[width:, :width]
    lower_right = factor_full[width:, width:]
    flat = rows.reshape(count * width, 2 * width)
    first = jax.scipy.linalg.solve_triangular(upper_left, flat[:, :width].T, lower=True).T
    reduced = flat[:, width:] - jnp.dot(first, lower_left.T, precision=lax.Precision.HIGHEST)
    second = jax.scipy.linalg.solve_triangular(lower_right, reduced.T, lower=True).T
    joined = jnp.concatenate([first, second], axis=1)
    return joined.reshape(count, width, 2 * width).astype(jnp.bfloat16)

def pair_product(rows_float, left_index, right_index):
    left_rows = jnp.take(rows_float, left_index, axis=0)
    right_rows = jnp.take(rows_float, right_index, axis=0)
    return jnp.einsum('tik,tjk->tij', left_rows, right_rows, precision=lax.Precision.HIGHEST)

def reference(diag_blocks, panel, local_targets, local_pairs, top_targets, top_pairs, top_pattern):
    groups = diag_blocks.shape[0]
    factors = [factor_group(diag_blocks[g], panel[g]) for g in range(groups)]
    panel_factor = jnp.stack(factors, axis=0)
    rows_all = panel_factor.astype(jnp.float32)
    width = panel.shape[2]
    local_list = []
    for g in range(groups):
        rows_float = rows_all[g]

        def slot_block(items):
            target_block, pair_block = items
            live = pair_block[:, 0] >= 0
            product = pair_product(rows_float, jnp.maximum(pair_block[:, 0], 0), jnp.maximum(pair_block[:, 1], 0))
            fresh = target_block.astype(jnp.float32) - jnp.where(live[:, None, None], product, jnp.float32(0.0))
            return fresh.astype(jnp.bfloat16)
        slots = local_targets.shape[1]
        blocked = lax.map(slot_block, (local_targets[g].reshape(slots // 8, 8, width, width), local_pairs[g].reshape(slots // 8, 8, 2)))
        local_list.append(blocked.reshape(slots, width, width))
    local_updated = jnp.stack(local_list, axis=0)

    def column(items):
        target_column, pair_column = items
        total = jnp.zeros(target_column.shape, jnp.float32)
        for g in range(groups):
            left_pos = jnp.take(top_pattern[g], pair_column[:, 0])
            right_pos = jnp.take(top_pattern[g], pair_column[:, 1])
            present = (left_pos >= 0) & (right_pos >= 0)
            product = pair_product(rows_all[g], jnp.maximum(left_pos, 0), jnp.maximum(right_pos, 0))
            total = total + jnp.where(present[:, None, None], product, jnp.float32(0.0))
        return (target_column.astype(jnp.float32) - total).astype(jnp.bfloat16)
    top_updated = lax.map(column, (top_targets, top_pairs))
    return (panel_factor, local_updated, top_updated)
```

```python
import functools

import jax
import jax.numpy as jnp
from jax import lax
from jax.experimental import pallas as pl
from jax.experimental.pallas import tpu as pltpu
from jax.sharding import Mesh
from jax.sharding import PartitionSpec as P


def _pair_kernel(k, has_targets, left_ref, right_ref, live_ref, *refs):
    lrefs = refs[:k]
    rrefs = refs[k:2 * k]
    out_ref = refs[-1]
    step = pl.program_id(0)
    for j in range(k):
        live = live_ref[step * k + j] > 0

        def product(j=j):
            return lax.dot_general(
                lrefs[j][0], rrefs[j][0], (((1,), (1,)), ((), ())),
                preferred_element_type=jnp.float32,
            )

        if has_targets:
            t_ref = refs[2 * k]

            @pl.when(live)
            def _(j=j):
                out_ref[j] = (t_ref[j].astype(jnp.float32) - product()).astype(out_ref.dtype)

            @pl.when(jnp.logical_not(live))
            def _(j=j):
                out_ref[j] = t_ref[j]
        else:

            @pl.when(live)
            def _(j=j):
                out_ref[j] = product().astype(out_ref.dtype)

            @pl.when(jnp.logical_not(live))
            def _(j=j):
                out_ref[j] = jnp.zeros(out_ref.shape[1:], out_ref.dtype)


def pair_products(rows_all, left, right, live, targets, k):
    count = left.shape[0]
    _, width, depth = rows_all.shape
    steps = count // k

    def row_map(j, which):
        def index(i, l_ref, r_ref, v_ref):
            ref = l_ref if which == 0 else r_ref
            return (ref[i * k + j], 0, 0)

        return index

    in_specs = [pl.BlockSpec((1, width, depth), row_map(j, 0)) for j in range(k)]
    in_specs += [pl.BlockSpec((1, width, depth), row_map(j, 1)) for j in range(k)]
    operands = [rows_all] * (2 * k)
    block_map = lambda i, l_ref, r_ref, v_ref: (i, 0, 0)
    if targets is not None:
        in_specs.append(pl.BlockSpec((k, width, width), block_map))
        operands.append(targets)
    grid_spec = pltpu.PrefetchScalarGridSpec(
        num_scalar_prefetch=3,
        grid=(steps,),
        in_specs=in_specs,
        out_specs=pl.BlockSpec((k, width, width), block_map),
    )
    flops = 2 * count * width * width * depth
    bytes_accessed = count * (2 * width * depth * 2 + 2 * width * width * 2)
    return pl.pallas_call(
        functools.partial(_pair_kernel, k, targets is not None),
        grid_spec=grid_spec,
        out_shape=jax.ShapeDtypeStruct((count, width, width), jnp.bfloat16),
        compiler_params=pltpu.CompilerParams(dimension_semantics=("arbitrary",)),
        cost_estimate=pl.CostEstimate(flops=flops, bytes_accessed=bytes_accessed, transcendentals=0),
    )(left, right, live, *operands)


def _step_of(count, limit=4):
    for k in range(limit, 0, -1):
        if count % k == 0:
            return k
    return 1


def on_device(n_chip, n_core, diag_blocks, panel, local_targets, local_pairs, top_targets, top_pairs, top_pattern):
    diagonal = diag_blocks[0]
    order = diagonal.shape[0]
    rows_local = panel[0]
    count, width, depth = rows_local.shape
    factor_full = jnp.linalg.cholesky(diagonal)
    inverse = jax.scipy.linalg.solve_triangular(
        factor_full, jnp.eye(order, dtype=jnp.float32), lower=True
    )
    flat = rows_local.reshape(count * width, depth)
    joined = jnp.dot(flat, inverse.T, precision=lax.Precision.HIGHEST)
    panel_here = joined.reshape(count, width, depth).astype(jnp.bfloat16)

    by_chip = lax.all_gather(panel_here, "chip", axis=0, tiled=True)
    rows_all = lax.all_gather(by_chip, "core", axis=0, tiled=True)

    def position(g):
        device = g // count
        return (device % n_core) * (n_chip * count) + (device // n_core) * count + g % count

    targets_here = local_targets[0]
    pairs_here = local_pairs[0]
    live = (pairs_here[:, 0] >= 0).astype(jnp.int32)
    left = position(jnp.maximum(pairs_here[:, 0], 0))
    right = position(jnp.maximum(pairs_here[:, 1], 0))
    slots = targets_here.shape[0]
    updated = pair_products(rows_all, left, right, live, targets_here, _step_of(slots))

    pattern = top_pattern[0]
    pairs_column = top_pairs[0]
    left_pos = jnp.take(pattern, pairs_column[:, 0], mode="clip")
    right_pos = jnp.take(pattern, pairs_column[:, 1], mode="clip")
    present = ((left_pos >= 0) & (right_pos >= 0)).astype(jnp.int32)
    top_count = pairs_column.shape[0]
    partial = pair_products(
        rows_all,
        position(jnp.maximum(left_pos, 0)),
        position(jnp.maximum(right_pos, 0)),
        present,
        None,
        _step_of(top_count),
    )
    summed = lax.psum_scatter(partial, "leaf", scatter_dimension=0, tiled=True).astype(jnp.float32)
    top_out = (top_targets[0].astype(jnp.float32) - summed).astype(jnp.bfloat16)[None]
    return (panel_here[None], updated[None], top_out)


def solution(mesh):
    n_leaf, n_blk = mesh.devices.shape
    n_core = 2 if n_blk % 2 == 0 else 1
    n_chip = n_blk // n_core
    split = Mesh(mesh.devices.reshape(n_leaf, n_chip, n_core), ("leaf", "chip", "core"))
    blk = ("chip", "core")
    in_specs = (
        P("leaf", None, None),
        P("leaf", blk, None, None),
        P("leaf", blk, None, None),
        P("leaf", blk, None),
        P(blk, "leaf", None, None),
        P(blk, None, None),
        P("leaf", None),
    )
    out_specs = (
        P("leaf", blk, None, None),
        P("leaf", blk, None, None),
        P(blk, "leaf", None, None),
    )
    return jax.shard_map(
        functools.partial(on_device, n_chip, n_core),
        mesh=split, in_specs=in_specs, out_specs=out_specs, check_vma=False,
    )
```

```python
import functools

import jax
import jax.numpy as jnp
from jax import lax
from jax.experimental import pallas as pl
from jax.experimental.pallas import tpu as pltpu
from jax.sharding import PartitionSpec as P


def _pair_kernel(k, has_targets, left_ref, right_ref, live_ref, *refs):
    lrefs = refs[:k]
    rrefs = refs[k:2 * k]
    out_ref = refs[-1]
    step = pl.program_id(0)
    for j in range(k):
        live = live_ref[step * k + j] > 0

        def product(j=j):
            return lax.dot_general(
                lrefs[j][0], rrefs[j][0], (((1,), (1,)), ((), ())),
                preferred_element_type=jnp.float32,
            )

        if has_targets:
            t_ref = refs[2 * k]

            @pl.when(live)
            def _(j=j):
                out_ref[j] = (t_ref[j].astype(jnp.float32) - product()).astype(out_ref.dtype)

            @pl.when(jnp.logical_not(live))
            def _(j=j):
                out_ref[j] = t_ref[j]
        else:

            @pl.when(live)
            def _(j=j):
                out_ref[j] = product().astype(out_ref.dtype)

            @pl.when(jnp.logical_not(live))
            def _(j=j):
                out_ref[j] = jnp.zeros(out_ref.shape[1:], out_ref.dtype)


def pair_products(rows_all, left, right, live, targets, k):
    count = left.shape[0]
    _, width, depth = rows_all.shape
    steps = count // k

    def row_map(j, which):
        def index(i, l_ref, r_ref, v_ref):
            ref = l_ref if which == 0 else r_ref
            return (ref[i * k + j], 0, 0)

        return index

    in_specs = [pl.BlockSpec((1, width, depth), row_map(j, 0)) for j in range(k)]
    in_specs += [pl.BlockSpec((1, width, depth), row_map(j, 1)) for j in range(k)]
    operands = [rows_all] * (2 * k)
    block_map = lambda i, l_ref, r_ref, v_ref: (i, 0, 0)
    if targets is not None:
        in_specs.append(pl.BlockSpec((k, width, width), block_map))
        operands.append(targets)
    grid_spec = pltpu.PrefetchScalarGridSpec(
        num_scalar_prefetch=3,
        grid=(steps,),
        in_specs=in_specs,
        out_specs=pl.BlockSpec((k, width, width), block_map),
    )
    flops = 2 * count * width * width * depth
    bytes_accessed = count * (2 * width * depth * 2 + 2 * width * width * 2)
    return pl.pallas_call(
        functools.partial(_pair_kernel, k, targets is not None),
        grid_spec=grid_spec,
        out_shape=jax.ShapeDtypeStruct((count, width, width), jnp.bfloat16),
        compiler_params=pltpu.CompilerParams(dimension_semantics=("arbitrary",)),
        cost_estimate=pl.CostEstimate(flops=flops, bytes_accessed=bytes_accessed, transcendentals=0),
    )(left, right, live, *operands)


def _step_of(count, limit=4):
    for k in range(limit, 0, -1):
        if count % k == 0:
            return k
    return 1

def _dot(a, b):
    return jnp.dot(a, b, precision=lax.Precision.HIGHEST)


def _inverse_factor(matrix, block):
    order = matrix.shape[0]
    nb = order // block
    eye = jnp.eye(block, dtype=matrix.dtype)
    trailing = matrix
    factor = {}
    diag_inv = []
    for k in range(nb):
        head = trailing[:block, :block]
        l_kk = jnp.linalg.cholesky(head)
        inv_kk = jax.scipy.linalg.solve_triangular(l_kk, eye, lower=True)
        diag_inv.append(inv_kk)
        if k + 1 < nb:
            below = _dot(trailing[block:, :block], inv_kk.T)
            for i in range(k + 1, nb):
                factor[(i, k)] = below[(i - k - 1) * block:(i - k) * block]
            trailing = trailing[block:, block:] - _dot(below, below.T)

    def inverse_of(lo, hi):
        if hi - lo == 1:
            return diag_inv[lo]
        mid = (lo + hi) // 2
        upper = inverse_of(lo, mid)
        lower = inverse_of(mid, hi)
        coupling = jnp.concatenate(
            [jnp.concatenate([factor[(i, j)] for j in range(lo, mid)], axis=1) for i in range(mid, hi)],
            axis=0,
        )
        corner = -_dot(lower, _dot(coupling, upper))
        top = jnp.concatenate([upper, jnp.zeros((upper.shape[0], lower.shape[1]), upper.dtype)], axis=1)
        bottom = jnp.concatenate([corner, lower], axis=1)
        return jnp.concatenate([top, bottom], axis=0)

    return inverse_of(0, nb)


def on_device(diag_blocks, panel, local_targets, local_pairs, top_targets, top_pairs, top_pattern):
    diagonal = diag_blocks[0]
    order = diagonal.shape[0]
    rows_local = panel[0]
    count, width, depth = rows_local.shape
    inverse = _inverse_factor(diagonal, 128)
    flat = rows_local.reshape(count * width, depth)
    joined = jnp.dot(flat, inverse.T, precision=lax.Precision.HIGHEST)
    panel_here = joined.reshape(count, width, depth).astype(jnp.bfloat16)

    rows_all = lax.all_gather(panel_here, "blk", axis=0, tiled=True)

    def position(g):
        return g

    targets_here = local_targets[0]
    pairs_here = local_pairs[0]
    live = (pairs_here[:, 0] >= 0).astype(jnp.int32)
    left = position(jnp.maximum(pairs_here[:, 0], 0))
    right = position(jnp.maximum(pairs_here[:, 1], 0))
    slots = targets_here.shape[0]
    updated = pair_products(rows_all, left, right, live, targets_here, _step_of(slots))

    pattern = top_pattern[0]
    pairs_column = top_pairs[0]
    left_pos = jnp.take(pattern, pairs_column[:, 0], mode="clip")
    right_pos = jnp.take(pattern, pairs_column[:, 1], mode="clip")
    present = ((left_pos >= 0) & (right_pos >= 0)).astype(jnp.int32)
    top_count = pairs_column.shape[0]
    partial = pair_products(
        rows_all,
        position(jnp.maximum(left_pos, 0)),
        position(jnp.maximum(right_pos, 0)),
        present,
        None,
        _step_of(top_count),
    )
    summed = lax.psum_scatter(partial, "leaf", scatter_dimension=0, tiled=True).astype(jnp.float32)
    top_out = (top_targets[0].astype(jnp.float32) - summed).astype(jnp.bfloat16)[None]
    return (panel_here[None], updated[None], top_out)


def solution(mesh):
    in_specs = (
        P("leaf", None, None),
        P("leaf", "blk", None, None),
        P("leaf", "blk", None, None),
        P("leaf", "blk", None),
        P("blk", "leaf", None, None),
        P("blk", None, None),
        P("leaf", None),
    )
    out_specs = (
        P("leaf", "blk", None, None),
        P("leaf", "blk", None, None),
        P("blk", "leaf", None, None),
    )
    return jax.shard_map(on_device, mesh=mesh, in_specs=in_specs, out_specs=out_specs, check_vma=False)
```

```python
import functools

import jax
import jax.numpy as jnp
from jax import lax
from jax.experimental import pallas as pl
from jax.experimental.pallas import tpu as pltpu
from jax.sharding import PartitionSpec as P


def _pair_kernel(k, chunks, has_targets, left_ref, right_ref, live_ref, *refs):
    per_slot = 2 * chunks
    out_ref = refs[-1]
    step = pl.program_id(0)
    for j in range(k):
        live = live_ref[step * k + j] > 0
        row_refs = refs[j * per_slot:(j + 1) * per_slot]

        def product(row_refs=row_refs):
            total = None
            for c in range(chunks):
                term = lax.dot_general(
                    row_refs[c][0], row_refs[chunks + c][0], (((1,), (1,)), ((), ())),
                    preferred_element_type=jnp.float32,
                )
                total = term if total is None else total + term
            return total

        if has_targets:
            t_ref = refs[k * per_slot]

            @pl.when(live)
            def _(j=j, product=product):
                out_ref[j] = (t_ref[j].astype(jnp.float32) - product()).astype(out_ref.dtype)

            @pl.when(jnp.logical_not(live))
            def _(j=j):
                out_ref[j] = t_ref[j]
        else:

            @pl.when(live)
            def _(j=j, product=product):
                out_ref[j] = product().astype(out_ref.dtype)

            @pl.when(jnp.logical_not(live))
            def _(j=j):
                out_ref[j] = jnp.zeros(out_ref.shape[1:], out_ref.dtype)


def pair_products(row_chunks, left, right, live, targets, k):
    count = left.shape[0]
    chunks = len(row_chunks)
    width = row_chunks[0].shape[1]
    steps = count // k

    def row_map(j, which):
        def index(i, l_ref, r_ref, v_ref):
            ref = l_ref if which == 0 else r_ref
            return (ref[i * k + j], 0, 0)

        return index

    in_specs = []
    operands = []
    for j in range(k):
        for which in (0, 1):
            for chunk in row_chunks:
                in_specs.append(pl.BlockSpec((1, width, chunk.shape[2]), row_map(j, which)))
                operands.append(chunk)
    block_map = lambda i, l_ref, r_ref, v_ref: (i, 0, 0)
    if targets is not None:
        in_specs.append(pl.BlockSpec((k, width, width), block_map))
        operands.append(targets)
    grid_spec = pltpu.PrefetchScalarGridSpec(
        num_scalar_prefetch=3,
        grid=(steps,),
        in_specs=in_specs,
        out_specs=pl.BlockSpec((k, width, width), block_map),
    )
    depth = sum(chunk.shape[2] for chunk in row_chunks)
    flops = 2 * count * width * width * depth
    bytes_accessed = count * (2 * width * depth * 2 + 2 * width * width * 2)
    return pl.pallas_call(
        functools.partial(_pair_kernel, k, chunks, targets is not None),
        grid_spec=grid_spec,
        out_shape=jax.ShapeDtypeStruct((count, width, width), jnp.bfloat16),
        compiler_params=pltpu.CompilerParams(dimension_semantics=("arbitrary",)),
        cost_estimate=pl.CostEstimate(flops=flops, bytes_accessed=bytes_accessed, transcendentals=0),
    )(left, right, live, *operands)


def _step_of(count, limit=4):
    for k in range(limit, 0, -1):
        if count % k == 0:
            return k
    return 1

def _dot(a, b):
    return jnp.dot(a, b, precision=lax.Precision.HIGHEST)


def _factor_row_blocks(matrix, block):
    order = matrix.shape[0]
    nb = order // block
    eye = jnp.eye(block, dtype=matrix.dtype)
    trailing = matrix
    factor = {}
    inverse = {}
    rows = []
    for k in range(nb):
        head = trailing[:block, :block]
        l_kk = jnp.linalg.cholesky(head)
        inv_kk = jax.scipy.linalg.solve_triangular(l_kk, eye, lower=True)
        inverse[(k, k)] = inv_kk
        for j in range(k):
            acc = None
            for m in range(j, k):
                term = _dot(factor[(k, m)], inverse[(m, j)])
                acc = term if acc is None else acc + term
            inverse[(k, j)] = -_dot(inv_kk, acc)
        rows.append(jnp.concatenate([inverse[(k, j)] for j in range(k + 1)], axis=1))
        if k + 1 < nb:
            below = _dot(trailing[block:, :block], inv_kk.T)
            for i in range(k + 1, nb):
                factor[(i, k)] = below[(i - k - 1) * block:(i - k) * block]
            trailing = trailing[block:, block:] - _dot(below, below.T)
    return rows


def on_device(diag_blocks, panel, local_targets, local_pairs, top_targets, top_pairs, top_pattern):
    diagonal = diag_blocks[0]
    order = diagonal.shape[0]
    rows_local = panel[0]
    count, width, depth = rows_local.shape
    block = 128
    inverse_rows = _factor_row_blocks(diagonal, block)
    flat = rows_local.reshape(count * width, depth)
    pieces = []
    gathered = []
    for k, inverse_row in enumerate(inverse_rows):
        source = flat
        if k >= 2:
            _, source = lax.optimization_barrier((gathered[k - 2], flat))
        piece = _dot(source[:, :(k + 1) * block], inverse_row.T).astype(jnp.bfloat16)
        piece = piece.reshape(count, width, block)
        pieces.append(piece)
        gathered.append(lax.all_gather(piece, "blk", axis=0, tiled=True))
    panel_here = jnp.concatenate(pieces, axis=2)

    def position(g):
        return g

    targets_here = local_targets[0]
    pairs_here = local_pairs[0]
    live = (pairs_here[:, 0] >= 0).astype(jnp.int32)
    left = position(jnp.maximum(pairs_here[:, 0], 0))
    right = position(jnp.maximum(pairs_here[:, 1], 0))
    slots = targets_here.shape[0]
    updated = pair_products(gathered, left, right, live, targets_here, _step_of(slots))

    pattern = top_pattern[0]
    pairs_column = top_pairs[0]
    left_pos = jnp.take(pattern, pairs_column[:, 0], mode="clip")
    right_pos = jnp.take(pattern, pairs_column[:, 1], mode="clip")
    present = ((left_pos >= 0) & (right_pos >= 0)).astype(jnp.int32)
    top_count = pairs_column.shape[0]
    partial = pair_products(
        gathered,
        position(jnp.maximum(left_pos, 0)),
        position(jnp.maximum(right_pos, 0)),
        present,
        None,
        _step_of(top_count),
    )
    summed = lax.psum_scatter(partial, "leaf", scatter_dimension=0, tiled=True).astype(jnp.float32)
    top_out = (top_targets[0].astype(jnp.float32) - summed).astype(jnp.bfloat16)[None]
    return (panel_here[None], updated[None], top_out)


def solution(mesh):
    in_specs = (
        P("leaf", None, None),
        P("leaf", "blk", None, None),
        P("leaf", "blk", None, None),
        P("leaf", "blk", None),
        P("blk", "leaf", None, None),
        P("blk", None, None),
        P("leaf", None),
    )
    out_specs = (
        P("leaf", "blk", None, None),
        P("leaf", "blk", None, None),
        P("blk", "leaf", None, None),
    )
    return jax.shard_map(on_device, mesh=mesh, in_specs=in_specs, out_specs=out_specs, check_vma=False)
```

```python
import functools

import jax
import jax.numpy as jnp
from jax import lax
from jax.experimental import pallas as pl
from jax.experimental.pallas import tpu as pltpu
from jax.sharding import PartitionSpec as P


def _pair_kernel(k, chunks, has_targets, left_ref, right_ref, live_ref, *refs):
    per_slot = 2 * chunks
    out_ref = refs[-1]
    step = pl.program_id(0)
    for j in range(k):
        live = live_ref[step * k + j] > 0
        row_refs = refs[j * per_slot:(j + 1) * per_slot]

        def product(row_refs=row_refs):
            total = None
            for c in range(chunks):
                term = lax.dot_general(
                    row_refs[c][0], row_refs[chunks + c][0], (((1,), (1,)), ((), ())),
                    preferred_element_type=jnp.float32,
                )
                total = term if total is None else total + term
            return total

        if has_targets:
            t_ref = refs[k * per_slot]

            @pl.when(live)
            def _(j=j, product=product):
                out_ref[j] = (t_ref[j].astype(jnp.float32) - product()).astype(out_ref.dtype)

            @pl.when(jnp.logical_not(live))
            def _(j=j):
                out_ref[j] = t_ref[j]
        else:

            @pl.when(live)
            def _(j=j, product=product):
                out_ref[j] = product().astype(out_ref.dtype)

            @pl.when(jnp.logical_not(live))
            def _(j=j):
                out_ref[j] = jnp.zeros(out_ref.shape[1:], out_ref.dtype)


def pair_products(row_chunks, left, right, live, targets, k):
    count = left.shape[0]
    chunks = len(row_chunks)
    width = row_chunks[0].shape[1]
    steps = count // k

    def row_map(j, which):
        def index(i, l_ref, r_ref, v_ref):
            ref = l_ref if which == 0 else r_ref
            return (ref[i * k + j], 0, 0)

        return index

    in_specs = []
    operands = []
    for j in range(k):
        for which in (0, 1):
            for chunk in row_chunks:
                in_specs.append(pl.BlockSpec((1, width, chunk.shape[2]), row_map(j, which)))
                operands.append(chunk)
    block_map = lambda i, l_ref, r_ref, v_ref: (i, 0, 0)
    if targets is not None:
        in_specs.append(pl.BlockSpec((k, width, width), block_map))
        operands.append(targets)
    grid_spec = pltpu.PrefetchScalarGridSpec(
        num_scalar_prefetch=3,
        grid=(steps,),
        in_specs=in_specs,
        out_specs=pl.BlockSpec((k, width, width), block_map),
    )
    depth = sum(chunk.shape[2] for chunk in row_chunks)
    flops = 2 * count * width * width * depth
    bytes_accessed = count * (2 * width * depth * 2 + 2 * width * width * 2)
    return pl.pallas_call(
        functools.partial(_pair_kernel, k, chunks, targets is not None),
        grid_spec=grid_spec,
        out_shape=jax.ShapeDtypeStruct((count, width, width), jnp.bfloat16),
        compiler_params=pltpu.CompilerParams(dimension_semantics=("arbitrary",)),
        cost_estimate=pl.CostEstimate(flops=flops, bytes_accessed=bytes_accessed, transcendentals=0),
    )(left, right, live, *operands)


def _step_of(count, limit=4):
    for k in range(limit, 0, -1):
        if count % k == 0:
            return k
    return 1

def _dot(a, b):
    return jnp.dot(a, b, precision=lax.Precision.HIGHEST)


def _factor_row_blocks(matrix, block):
    order = matrix.shape[0]
    nb = order // block
    eye = jnp.eye(block, dtype=matrix.dtype)
    trailing = matrix
    factor = {}
    inverse = {}
    rows = []
    for k in range(nb):
        head = trailing[:block, :block]
        l_kk = jnp.linalg.cholesky(head)
        inv_kk = jax.scipy.linalg.solve_triangular(l_kk, eye, lower=True)
        inverse[(k, k)] = inv_kk
        for j in range(k):
            acc = None
            for m in range(j, k):
                term = _dot(factor[(k, m)], inverse[(m, j)])
                acc = term if acc is None else acc + term
            inverse[(k, j)] = -_dot(inv_kk, acc)
        rows.append(jnp.concatenate([inverse[(k, j)] for j in range(k + 1)], axis=1))
        if k + 1 < nb:
            below = _dot(trailing[block:, :block], inv_kk.T)
            for i in range(k + 1, nb):
                factor[(i, k)] = below[(i - k - 1) * block:(i - k) * block]
            trailing = trailing[block:, block:] - _dot(below, below.T)
    return rows


def on_device(diag_blocks, panel, local_targets, local_pairs, top_targets, top_pairs, top_pattern):
    diagonal = diag_blocks[0]
    order = diagonal.shape[0]
    rows_local = panel[0]
    count, width, depth = rows_local.shape
    block = 128
    inverse_rows = _factor_row_blocks(diagonal, block)
    flat = rows_local.reshape(count * width, depth)
    groups = ((0, 2), (2, len(inverse_rows)))
    pieces = []
    gathered = []
    for p, (lo, hi) in enumerate(groups):
        source = flat
        if p >= 1:
            _, source = lax.optimization_barrier((gathered[p - 1], flat))
        columns = [
            _dot(source[:, :(k + 1) * block], inverse_rows[k].T).astype(jnp.bfloat16)
            for k in range(lo, hi)
        ]
        piece = jnp.concatenate(columns, axis=1).reshape(count, width, (hi - lo) * block)
        pieces.append(piece)
        gathered.append(lax.all_gather(piece, "blk", axis=0, tiled=True))
    panel_here = jnp.concatenate(pieces, axis=2)

    def position(g):
        return g

    targets_here = local_targets[0]
    pairs_here = local_pairs[0]
    live = (pairs_here[:, 0] >= 0).astype(jnp.int32)
    left = position(jnp.maximum(pairs_here[:, 0], 0))
    right = position(jnp.maximum(pairs_here[:, 1], 0))
    slots = targets_here.shape[0]
    updated = pair_products(gathered, left, right, live, targets_here, _step_of(slots))

    pattern = top_pattern[0]
    pairs_column = top_pairs[0]
    left_pos = jnp.take(pattern, pairs_column[:, 0], mode="clip")
    right_pos = jnp.take(pattern, pairs_column[:, 1], mode="clip")
    present = ((left_pos >= 0) & (right_pos >= 0)).astype(jnp.int32)
    top_count = pairs_column.shape[0]
    partial = pair_products(
        gathered,
        position(jnp.maximum(left_pos, 0)),
        position(jnp.maximum(right_pos, 0)),
        present,
        None,
        _step_of(top_count),
    )
    summed = lax.psum_scatter(partial, "leaf", scatter_dimension=0, tiled=True).astype(jnp.float32)
    top_out = (top_targets[0].astype(jnp.float32) - summed).astype(jnp.bfloat16)[None]
    return (panel_here[None], updated[None], top_out)


def solution(mesh):
    in_specs = (
        P("leaf", None, None),
        P("leaf", "blk", None, None),
        P("leaf", "blk", None, None),
        P("leaf", "blk", None),
        P("blk", "leaf", None, None),
        P("blk", None, None),
        P("leaf", None),
    )
    out_specs = (
        P("leaf", "blk", None, None),
        P("leaf", "blk", None, None),
        P("blk", "leaf", None, None),
    )
    return jax.shard_map(on_device, mesh=mesh, in_specs=in_specs, out_specs=out_specs, check_vma=False)
```

```python
import functools

import jax
import jax.numpy as jnp
from jax import lax
from jax.experimental import pallas as pl
from jax.experimental.pallas import tpu as pltpu
from jax.sharding import PartitionSpec as P


def _pair_kernel(k, has_targets, left_ref, right_ref, live_ref, *refs):
    lrefs = refs[:k]
    rrefs = refs[k:2 * k]
    out_ref = refs[-1]
    step = pl.program_id(0)
    for j in range(k):
        live = live_ref[step * k + j] > 0

        def product(j=j):
            return lax.dot_general(
                lrefs[j][0], rrefs[j][0], (((1,), (1,)), ((), ())),
                preferred_element_type=jnp.float32,
            )

        if has_targets:
            t_ref = refs[2 * k]

            @pl.when(live)
            def _(j=j):
                out_ref[j] = (t_ref[j].astype(jnp.float32) - product()).astype(out_ref.dtype)

            @pl.when(jnp.logical_not(live))
            def _(j=j):
                out_ref[j] = t_ref[j]
        else:

            @pl.when(live)
            def _(j=j):
                out_ref[j] = product().astype(out_ref.dtype)

            @pl.when(jnp.logical_not(live))
            def _(j=j):
                out_ref[j] = jnp.zeros(out_ref.shape[1:], out_ref.dtype)


def pair_products(rows_all, left, right, live, targets, k):
    count = left.shape[0]
    _, width, depth = rows_all.shape
    steps = count // k

    def row_map(j, which):
        def index(i, l_ref, r_ref, v_ref):
            ref = l_ref if which == 0 else r_ref
            return (ref[i * k + j], 0, 0)

        return index

    in_specs = [pl.BlockSpec((1, width, depth), row_map(j, 0)) for j in range(k)]
    in_specs += [pl.BlockSpec((1, width, depth), row_map(j, 1)) for j in range(k)]
    operands = [rows_all] * (2 * k)
    block_map = lambda i, l_ref, r_ref, v_ref: (i, 0, 0)
    if targets is not None:
        in_specs.append(pl.BlockSpec((k, width, width), block_map))
        operands.append(targets)
    grid_spec = pltpu.PrefetchScalarGridSpec(
        num_scalar_prefetch=3,
        grid=(steps,),
        in_specs=in_specs,
        out_specs=pl.BlockSpec((k, width, width), block_map),
    )
    flops = 2 * count * width * width * depth
    bytes_accessed = count * (2 * width * depth * 2 + 2 * width * width * 2)
    return pl.pallas_call(
        functools.partial(_pair_kernel, k, targets is not None),
        grid_spec=grid_spec,
        out_shape=jax.ShapeDtypeStruct((count, width, width), jnp.bfloat16),
        compiler_params=pltpu.CompilerParams(dimension_semantics=("arbitrary",)),
        cost_estimate=pl.CostEstimate(flops=flops, bytes_accessed=bytes_accessed, transcendentals=0),
    )(left, right, live, *operands)


def _step_of(count, limit=4):
    for k in range(limit, 0, -1):
        if count % k == 0:
            return k
    return 1

def _dot(a, b):
    return jnp.dot(a, b, precision=lax.Precision.HIGHEST)


def _inverse_factor(matrix, block):
    order = matrix.shape[0]
    nb = order // block
    eye = jnp.eye(block, dtype=matrix.dtype)
    trailing = matrix
    factor = {}
    diag_inv = []
    for k in range(nb):
        head = trailing[:block, :block]
        l_kk = jnp.linalg.cholesky(head)
        inv_kk = jax.scipy.linalg.solve_triangular(l_kk, eye, lower=True)
        diag_inv.append(inv_kk)
        if k + 1 < nb:
            below = _dot(trailing[block:, :block], inv_kk.T)
            for i in range(k + 1, nb):
                factor[(i, k)] = below[(i - k - 1) * block:(i - k) * block]
            trailing = trailing[block:, block:] - _dot(below, below.T)

    def inverse_of(lo, hi):
        if hi - lo == 1:
            return diag_inv[lo]
        mid = (lo + hi) // 2
        upper = inverse_of(lo, mid)
        lower = inverse_of(mid, hi)
        coupling = jnp.concatenate(
            [jnp.concatenate([factor[(i, j)] for j in range(lo, mid)], axis=1) for i in range(mid, hi)],
            axis=0,
        )
        corner = -_dot(lower, _dot(coupling, upper))
        top = jnp.concatenate([upper, jnp.zeros((upper.shape[0], lower.shape[1]), upper.dtype)], axis=1)
        bottom = jnp.concatenate([corner, lower], axis=1)
        return jnp.concatenate([top, bottom], axis=0)

    return inverse_of(0, nb)


def on_device(diag_blocks, panel, local_targets, local_pairs, top_targets, top_pairs, top_pattern):
    diagonal = diag_blocks[0]
    order = diagonal.shape[0]
    rows_local = panel[0]
    count, width, depth = rows_local.shape
    inverse = _inverse_factor(diagonal, 128)
    flat = rows_local.reshape(count * width, depth)
    joined = jnp.dot(flat, inverse.T, precision=lax.Precision.HIGHEST)
    panel_here = joined.reshape(count, width, depth).astype(jnp.bfloat16)

    rows_all = lax.all_gather(panel_here, "blk", axis=0, tiled=True)

    def position(g):
        return g

    targets_here = local_targets[0]
    pairs_here = local_pairs[0]
    live = (pairs_here[:, 0] >= 0).astype(jnp.int32)
    left = position(jnp.maximum(pairs_here[:, 0], 0))
    right = position(jnp.maximum(pairs_here[:, 1], 0))
    slots = targets_here.shape[0]
    updated = pair_products(rows_all, left, right, live, targets_here, _step_of(slots))

    pattern = top_pattern[0]
    pairs_column = top_pairs[0]
    left_pos = jnp.take(pattern, pairs_column[:, 0], mode="clip")
    right_pos = jnp.take(pattern, pairs_column[:, 1], mode="clip")
    present = ((left_pos >= 0) & (right_pos >= 0)).astype(jnp.int32)
    top_count = pairs_column.shape[0]
    partial = pair_products(
        rows_all,
        position(jnp.maximum(left_pos, 0)),
        position(jnp.maximum(right_pos, 0)),
        present,
        None,
        _step_of(top_count),
    )
    n_leaf = lax.axis_size("leaf")
    me = lax.axis_index("leaf")
    own = top_count // n_leaf
    summed = lax.dynamic_slice_in_dim(partial, me * own, own, 0).astype(jnp.float32)
    for shift in range(1, n_leaf):
        outgoing = lax.dynamic_slice_in_dim(partial, ((me + shift) % n_leaf) * own, own, 0)
        arrived = lax.ppermute(
            outgoing, "leaf", [(i, (i + shift) % n_leaf) for i in range(n_leaf)]
        )
        summed = summed + arrived.astype(jnp.float32)
    top_out = (top_targets[0].astype(jnp.float32) - summed).astype(jnp.bfloat16)[None]
    return (panel_here[None], updated[None], top_out)


def solution(mesh):
    in_specs = (
        P("leaf", None, None),
        P("leaf", "blk", None, None),
        P("leaf", "blk", None, None),
        P("leaf", "blk", None),
        P("blk", "leaf", None, None),
        P("blk", None, None),
        P("leaf", None),
    )
    out_specs = (
        P("leaf", "blk", None, None),
        P("leaf", "blk", None, None),
        P("blk", "leaf", None, None),
    )
    return jax.shard_map(on_device, mesh=mesh, in_specs=in_specs, out_specs=out_specs, check_vma=False)
```

```python
import functools

import jax
import jax.numpy as jnp
from jax import lax
from jax.experimental import pallas as pl
from jax.experimental.pallas import tpu as pltpu
from jax.sharding import PartitionSpec as P


def _pair_kernel(k, has_targets, left_ref, right_ref, live_ref, *refs):
    lrefs = refs[:k]
    rrefs = refs[k:2 * k]
    out_ref = refs[-1]
    step = pl.program_id(0)
    for j in range(k):
        live = live_ref[step * k + j] > 0

        def product(j=j):
            return lax.dot_general(
                lrefs[j][0], rrefs[j][0], (((1,), (1,)), ((), ())),
                preferred_element_type=jnp.float32,
            )

        if has_targets:
            t_ref = refs[2 * k]

            @pl.when(live)
            def _(j=j):
                out_ref[j] = (t_ref[j].astype(jnp.float32) - product()).astype(out_ref.dtype)

            @pl.when(jnp.logical_not(live))
            def _(j=j):
                out_ref[j] = t_ref[j]
        else:

            @pl.when(live)
            def _(j=j):
                out_ref[j] = product().astype(out_ref.dtype)

            @pl.when(jnp.logical_not(live))
            def _(j=j):
                out_ref[j] = jnp.zeros(out_ref.shape[1:], out_ref.dtype)


def pair_products(rows_all, left, right, live, targets, k):
    count = left.shape[0]
    _, width, depth = rows_all.shape
    steps = count // k

    def row_map(j, which):
        def index(i, l_ref, r_ref, v_ref):
            ref = l_ref if which == 0 else r_ref
            return (ref[i * k + j], 0, 0)

        return index

    in_specs = [pl.BlockSpec((1, width, depth), row_map(j, 0)) for j in range(k)]
    in_specs += [pl.BlockSpec((1, width, depth), row_map(j, 1)) for j in range(k)]
    operands = [rows_all] * (2 * k)
    block_map = lambda i, l_ref, r_ref, v_ref: (i, 0, 0)
    if targets is not None:
        in_specs.append(pl.BlockSpec((k, width, width), block_map))
        operands.append(targets)
    grid_spec = pltpu.PrefetchScalarGridSpec(
        num_scalar_prefetch=3,
        grid=(steps,),
        in_specs=in_specs,
        out_specs=pl.BlockSpec((k, width, width), block_map),
    )
    flops = 2 * count * width * width * depth
    bytes_accessed = count * (2 * width * depth * 2 + 2 * width * width * 2)
    return pl.pallas_call(
        functools.partial(_pair_kernel, k, targets is not None),
        grid_spec=grid_spec,
        out_shape=jax.ShapeDtypeStruct((count, width, width), jnp.bfloat16),
        compiler_params=pltpu.CompilerParams(dimension_semantics=("arbitrary",)),
        cost_estimate=pl.CostEstimate(flops=flops, bytes_accessed=bytes_accessed, transcendentals=0),
    )(left, right, live, *operands)


def _resident_kernel(k, left_ref, right_ref, live_ref, rows_hbm, t_ref, out_ref, rows_vmem, sem):
    step = pl.program_id(0)

    @pl.when(step == 0)
    def _():
        copy = pltpu.make_async_copy(rows_hbm, rows_vmem, sem)
        copy.start()
        copy.wait()

    for j in range(k):
        slot = step * k + j
        live = live_ref[slot] > 0

        @pl.when(live)
        def _(j=j, slot=slot):
            product = lax.dot_general(
                rows_vmem[left_ref[slot]], rows_vmem[right_ref[slot]], (((1,), (1,)), ((), ())),
                preferred_element_type=jnp.float32,
            )
            out_ref[j] = (t_ref[j].astype(jnp.float32) - product).astype(out_ref.dtype)

        @pl.when(jnp.logical_not(live))
        def _(j=j):
            out_ref[j] = t_ref[j]


def resident_updates(rows_all, left, right, live, targets, k):
    count = left.shape[0]
    width = targets.shape[1]
    block_map = lambda i, l_ref, r_ref, v_ref: (i, 0, 0)
    grid_spec = pltpu.PrefetchScalarGridSpec(
        num_scalar_prefetch=3,
        grid=(count // k,),
        in_specs=[pl.BlockSpec(memory_space=pl.ANY), pl.BlockSpec((k, width, width), block_map)],
        out_specs=pl.BlockSpec((k, width, width), block_map),
        scratch_shapes=[pltpu.VMEM(rows_all.shape, rows_all.dtype), pltpu.SemaphoreType.DMA(())],
    )
    depth = rows_all.shape[2]
    flops = 2 * count * width * width * depth
    bytes_accessed = rows_all.size * 2 + count * 2 * width * width * 2
    return pl.pallas_call(
        functools.partial(_resident_kernel, k),
        grid_spec=grid_spec,
        out_shape=jax.ShapeDtypeStruct(targets.shape, targets.dtype),
        compiler_params=pltpu.CompilerParams(
            dimension_semantics=("arbitrary",), vmem_limit_bytes=56 * 1024 * 1024
        ),
        cost_estimate=pl.CostEstimate(flops=flops, bytes_accessed=bytes_accessed, transcendentals=0),
    )(left, right, live, rows_all, targets)


def _step_of(count, limit=4):
    for k in range(limit, 0, -1):
        if count % k == 0:
            return k
    return 1

def _dot(a, b):
    return jnp.dot(a, b, precision=lax.Precision.HIGHEST)


def _inverse_factor(matrix, block):
    order = matrix.shape[0]
    nb = order // block
    eye = jnp.eye(block, dtype=matrix.dtype)
    trailing = matrix
    factor = {}
    diag_inv = []
    for k in range(nb):
        head = trailing[:block, :block]
        l_kk = jnp.linalg.cholesky(head)
        inv_kk = jax.scipy.linalg.solve_triangular(l_kk, eye, lower=True)
        diag_inv.append(inv_kk)
        if k + 1 < nb:
            below = _dot(trailing[block:, :block], inv_kk.T)
            for i in range(k + 1, nb):
                factor[(i, k)] = below[(i - k - 1) * block:(i - k) * block]
            trailing = trailing[block:, block:] - _dot(below, below.T)

    def inverse_of(lo, hi):
        if hi - lo == 1:
            return diag_inv[lo]
        mid = (lo + hi) // 2
        upper = inverse_of(lo, mid)
        lower = inverse_of(mid, hi)
        coupling = jnp.concatenate(
            [jnp.concatenate([factor[(i, j)] for j in range(lo, mid)], axis=1) for i in range(mid, hi)],
            axis=0,
        )
        corner = -_dot(lower, _dot(coupling, upper))
        top = jnp.concatenate([upper, jnp.zeros((upper.shape[0], lower.shape[1]), upper.dtype)], axis=1)
        bottom = jnp.concatenate([corner, lower], axis=1)
        return jnp.concatenate([top, bottom], axis=0)

    return inverse_of(0, nb)


def on_device(diag_blocks, panel, local_targets, local_pairs, top_targets, top_pairs, top_pattern):
    diagonal = diag_blocks[0]
    order = diagonal.shape[0]
    rows_local = panel[0]
    count, width, depth = rows_local.shape
    inverse = _inverse_factor(diagonal, 128)
    flat = rows_local.reshape(count * width, depth)
    joined = jnp.dot(flat, inverse.T, precision=lax.Precision.HIGHEST)
    panel_here = joined.reshape(count, width, depth).astype(jnp.bfloat16)

    rows_all = lax.all_gather(panel_here, "blk", axis=0, tiled=True)

    def position(g):
        return g

    targets_here = local_targets[0]
    pairs_here = local_pairs[0]
    live = (pairs_here[:, 0] >= 0).astype(jnp.int32)
    last_row = rows_all.shape[0] - 1
    left = position(jnp.clip(pairs_here[:, 0], 0, last_row))
    right = position(jnp.clip(pairs_here[:, 1], 0, last_row))
    slots = targets_here.shape[0]
    updated = resident_updates(rows_all, left, right, live, targets_here, _step_of(slots))

    pattern = top_pattern[0]
    pairs_column = top_pairs[0]
    left_pos = jnp.take(pattern, pairs_column[:, 0], mode="clip")
    right_pos = jnp.take(pattern, pairs_column[:, 1], mode="clip")
    present = ((left_pos >= 0) & (right_pos >= 0)).astype(jnp.int32)
    top_count = pairs_column.shape[0]
    partial = pair_products(
        rows_all,
        position(jnp.maximum(left_pos, 0)),
        position(jnp.maximum(right_pos, 0)),
        present,
        None,
        _step_of(top_count),
    )
    summed = lax.psum_scatter(partial, "leaf", scatter_dimension=0, tiled=True).astype(jnp.float32)
    top_out = (top_targets[0].astype(jnp.float32) - summed).astype(jnp.bfloat16)[None]
    return (panel_here[None], updated[None], top_out)


def solution(mesh):
    in_specs = (
        P("leaf", None, None),
        P("leaf", "blk", None, None),
        P("leaf", "blk", None, None),
        P("leaf", "blk", None),
        P("blk", "leaf", None, None),
        P("blk", None, None),
        P("leaf", None),
    )
    out_specs = (
        P("leaf", "blk", None, None),
        P("leaf", "blk", None, None),
        P("blk", "leaf", None, None),
    )
    return jax.shard_map(on_device, mesh=mesh, in_specs=in_specs, out_specs=out_specs, check_vma=False)
```

```python
import functools

import jax
import jax.numpy as jnp
from jax import lax
from jax.experimental import pallas as pl
from jax.experimental.pallas import tpu as pltpu
from jax.sharding import PartitionSpec as P


def _pair_kernel(k, has_targets, left_ref, right_ref, live_ref, *refs):
    lrefs = refs[:k]
    rrefs = refs[k:2 * k]
    out_ref = refs[-1]
    step = pl.program_id(0)
    for j in range(k):
        live = live_ref[step * k + j] > 0

        def product(j=j):
            return lax.dot_general(
                lrefs[j][0], rrefs[j][0], (((1,), (1,)), ((), ())),
                preferred_element_type=jnp.float32,
            )

        if has_targets:
            t_ref = refs[2 * k]

            @pl.when(live)
            def _(j=j):
                out_ref[j] = (t_ref[j].astype(jnp.float32) - product()).astype(out_ref.dtype)

            @pl.when(jnp.logical_not(live))
            def _(j=j):
                out_ref[j] = t_ref[j]
        else:

            @pl.when(live)
            def _(j=j):
                out_ref[j] = product().astype(out_ref.dtype)

            @pl.when(jnp.logical_not(live))
            def _(j=j):
                out_ref[j] = jnp.zeros(out_ref.shape[1:], out_ref.dtype)


def pair_products(rows_all, left, right, live, targets, k):
    count = left.shape[0]
    _, width, depth = rows_all.shape
    steps = count // k

    def row_map(j, which):
        def index(i, l_ref, r_ref, v_ref):
            ref = l_ref if which == 0 else r_ref
            return (ref[i * k + j], 0, 0)

        return index

    in_specs = [pl.BlockSpec((1, width, depth), row_map(j, 0)) for j in range(k)]
    in_specs += [pl.BlockSpec((1, width, depth), row_map(j, 1)) for j in range(k)]
    operands = [rows_all] * (2 * k)
    block_map = lambda i, l_ref, r_ref, v_ref: (i, 0, 0)
    if targets is not None:
        in_specs.append(pl.BlockSpec((k, width, width), block_map))
        operands.append(targets)
    grid_spec = pltpu.PrefetchScalarGridSpec(
        num_scalar_prefetch=3,
        grid=(steps,),
        in_specs=in_specs,
        out_specs=pl.BlockSpec((k, width, width), block_map),
    )
    flops = 2 * count * width * width * depth
    bytes_accessed = count * (2 * width * depth * 2 + 2 * width * width * 2)
    return pl.pallas_call(
        functools.partial(_pair_kernel, k, targets is not None),
        grid_spec=grid_spec,
        out_shape=jax.ShapeDtypeStruct((count, width, width), jnp.bfloat16),
        compiler_params=pltpu.CompilerParams(dimension_semantics=("arbitrary",)),
        cost_estimate=pl.CostEstimate(flops=flops, bytes_accessed=bytes_accessed, transcendentals=0),
    )(left, right, live, *operands)


def _resident_kernel(k, left_ref, right_ref, live_ref, rows_hbm, t_ref, out_ref, rows_vmem, sem):
    step = pl.program_id(0)

    @pl.when(step == 0)
    def _():
        parts = sem.shape[0]
        size = rows_vmem.shape[0] // parts
        copies = [
            pltpu.make_async_copy(
                rows_hbm.at[pl.ds(c * size, size)], rows_vmem.at[pl.ds(c * size, size)], sem.at[c]
            )
            for c in range(parts)
        ]
        for copy in copies:
            copy.start()
        for copy in copies:
            copy.wait()

    for j in range(k):
        slot = step * k + j
        live = live_ref[slot] > 0

        @pl.when(live)
        def _(j=j, slot=slot):
            product = lax.dot_general(
                rows_vmem[left_ref[slot]], rows_vmem[right_ref[slot]], (((1,), (1,)), ((), ())),
                preferred_element_type=jnp.float32,
            )
            out_ref[j] = (t_ref[j].astype(jnp.float32) - product).astype(out_ref.dtype)

        @pl.when(jnp.logical_not(live))
        def _(j=j):
            out_ref[j] = t_ref[j]


def resident_updates(rows_all, left, right, live, targets, k):
    count = left.shape[0]
    width = targets.shape[1]
    block_map = lambda i, l_ref, r_ref, v_ref: (i, 0, 0)
    grid_spec = pltpu.PrefetchScalarGridSpec(
        num_scalar_prefetch=3,
        grid=(count // k,),
        in_specs=[pl.BlockSpec(memory_space=pl.ANY), pl.BlockSpec((k, width, width), block_map)],
        out_specs=pl.BlockSpec((k, width, width), block_map),
        scratch_shapes=[pltpu.VMEM(rows_all.shape, rows_all.dtype), pltpu.SemaphoreType.DMA((_parts_of(rows_all.shape[0]),))],
    )
    depth = rows_all.shape[2]
    flops = 2 * count * width * width * depth
    bytes_accessed = rows_all.size * 2 + count * 2 * width * width * 2
    return pl.pallas_call(
        functools.partial(_resident_kernel, k),
        grid_spec=grid_spec,
        out_shape=jax.ShapeDtypeStruct(targets.shape, targets.dtype),
        compiler_params=pltpu.CompilerParams(
            dimension_semantics=("arbitrary",), vmem_limit_bytes=56 * 1024 * 1024
        ),
        cost_estimate=pl.CostEstimate(flops=flops, bytes_accessed=bytes_accessed, transcendentals=0),
    )(left, right, live, rows_all, targets)


def _parts_of(rows, limit=8):
    for parts in range(limit, 0, -1):
        if rows % parts == 0:
            return parts
    return 1


def _step_of(count, limit=4):
    for k in range(limit, 0, -1):
        if count % k == 0:
            return k
    return 1

def _dot(a, b):
    return jnp.dot(a, b, precision=lax.Precision.HIGHEST)


def _inverse_factor(matrix, block):
    order = matrix.shape[0]
    nb = order // block
    eye = jnp.eye(block, dtype=matrix.dtype)
    trailing = matrix
    factor = {}
    diag_inv = []
    for k in range(nb):
        head = trailing[:block, :block]
        l_kk = jnp.linalg.cholesky(head)
        inv_kk = jax.scipy.linalg.solve_triangular(l_kk, eye, lower=True)
        diag_inv.append(inv_kk)
        if k + 1 < nb:
            below = _dot(trailing[block:, :block], inv_kk.T)
            for i in range(k + 1, nb):
                factor[(i, k)] = below[(i - k - 1) * block:(i - k) * block]
            trailing = trailing[block:, block:] - _dot(below, below.T)

    def inverse_of(lo, hi):
        if hi - lo == 1:
            return diag_inv[lo]
        mid = (lo + hi) // 2
        upper = inverse_of(lo, mid)
        lower = inverse_of(mid, hi)
        coupling = jnp.concatenate(
            [jnp.concatenate([factor[(i, j)] for j in range(lo, mid)], axis=1) for i in range(mid, hi)],
            axis=0,
        )
        corner = -_dot(lower, _dot(coupling, upper))
        top = jnp.concatenate([upper, jnp.zeros((upper.shape[0], lower.shape[1]), upper.dtype)], axis=1)
        bottom = jnp.concatenate([corner, lower], axis=1)
        return jnp.concatenate([top, bottom], axis=0)

    return inverse_of(0, nb)


def on_device(diag_blocks, panel, local_targets, local_pairs, top_targets, top_pairs, top_pattern):
    diagonal = diag_blocks[0]
    order = diagonal.shape[0]
    rows_local = panel[0]
    count, width, depth = rows_local.shape
    inverse = _inverse_factor(diagonal, 128)
    flat = rows_local.reshape(count * width, depth)
    joined = jnp.dot(flat, inverse.T, precision=lax.Precision.HIGHEST)
    panel_here = joined.reshape(count, width, depth).astype(jnp.bfloat16)

    rows_all = lax.all_gather(panel_here, "blk", axis=0, tiled=True)

    def position(g):
        return g

    targets_here = local_targets[0]
    pairs_here = local_pairs[0]
    live = (pairs_here[:, 0] >= 0).astype(jnp.int32)
    last_row = rows_all.shape[0] - 1
    left = position(jnp.clip(pairs_here[:, 0], 0, last_row))
    right = position(jnp.clip(pairs_here[:, 1], 0, last_row))
    slots = targets_here.shape[0]
    updated = resident_updates(rows_all, left, right, live, targets_here, _step_of(slots))

    pattern = top_pattern[0]
    pairs_column = top_pairs[0]
    left_pos = jnp.take(pattern, pairs_column[:, 0], mode="clip")
    right_pos = jnp.take(pattern, pairs_column[:, 1], mode="clip")
    present = ((left_pos >= 0) & (right_pos >= 0)).astype(jnp.int32)
    top_count = pairs_column.shape[0]
    partial = pair_products(
        rows_all,
        position(jnp.maximum(left_pos, 0)),
        position(jnp.maximum(right_pos, 0)),
        present,
        None,
        _step_of(top_count),
    )
    summed = lax.psum_scatter(partial, "leaf", scatter_dimension=0, tiled=True).astype(jnp.float32)
    top_out = (top_targets[0].astype(jnp.float32) - summed).astype(jnp.bfloat16)[None]
    return (panel_here[None], updated[None], top_out)


def solution(mesh):
    in_specs = (
        P("leaf", None, None),
        P("leaf", "blk", None, None),
        P("leaf", "blk", None, None),
        P("leaf", "blk", None),
        P("blk", "leaf", None, None),
        P("blk", None, None),
        P("leaf", None),
    )
    out_specs = (
        P("leaf", "blk", None, None),
        P("leaf", "blk", None, None),
        P("blk", "leaf", None, None),
    )
    return jax.shard_map(on_device, mesh=mesh, in_specs=in_specs, out_specs=out_specs, check_vma=False)
```

```python
import functools

import jax
import jax.numpy as jnp
from jax import lax
from jax.experimental import pallas as pl
from jax.experimental.pallas import tpu as pltpu
from jax.sharding import PartitionSpec as P


def _pair_kernel(k, has_targets, left_ref, right_ref, live_ref, *refs):
    lrefs = refs[:k]
    rrefs = refs[k:2 * k]
    out_ref = refs[-1]
    step = pl.program_id(0)
    for j in range(k):
        live = live_ref[step * k + j] > 0

        def product(j=j):
            return lax.dot_general(
                lrefs[j][0], rrefs[j][0], (((1,), (1,)), ((), ())),
                preferred_element_type=jnp.float32,
            )

        if has_targets:
            t_ref = refs[2 * k]

            @pl.when(live)
            def _(j=j):
                out_ref[j] = (t_ref[j].astype(jnp.float32) - product()).astype(out_ref.dtype)

            @pl.when(jnp.logical_not(live))
            def _(j=j):
                out_ref[j] = t_ref[j]
        else:

            @pl.when(live)
            def _(j=j):
                out_ref[j] = product().astype(out_ref.dtype)

            @pl.when(jnp.logical_not(live))
            def _(j=j):
                out_ref[j] = jnp.zeros(out_ref.shape[1:], out_ref.dtype)


def pair_products(rows_all, left, right, live, targets, k):
    count = left.shape[0]
    _, width, depth = rows_all.shape
    steps = count // k

    def row_map(j, which):
        def index(i, l_ref, r_ref, v_ref):
            ref = l_ref if which == 0 else r_ref
            return (ref[i * k + j], 0, 0)

        return index

    in_specs = [pl.BlockSpec((1, width, depth), row_map(j, 0)) for j in range(k)]
    in_specs += [pl.BlockSpec((1, width, depth), row_map(j, 1)) for j in range(k)]
    operands = [rows_all] * (2 * k)
    block_map = lambda i, l_ref, r_ref, v_ref: (i, 0, 0)
    if targets is not None:
        in_specs.append(pl.BlockSpec((k, width, width), block_map))
        operands.append(targets)
    grid_spec = pltpu.PrefetchScalarGridSpec(
        num_scalar_prefetch=3,
        grid=(steps,),
        in_specs=in_specs,
        out_specs=pl.BlockSpec((k, width, width), block_map),
    )
    flops = 2 * count * width * width * depth
    bytes_accessed = count * (2 * width * depth * 2 + 2 * width * width * 2)
    return pl.pallas_call(
        functools.partial(_pair_kernel, k, targets is not None),
        grid_spec=grid_spec,
        out_shape=jax.ShapeDtypeStruct((count, width, width), jnp.bfloat16),
        compiler_params=pltpu.CompilerParams(dimension_semantics=("arbitrary",)),
        cost_estimate=pl.CostEstimate(flops=flops, bytes_accessed=bytes_accessed, transcendentals=0),
    )(left, right, live, *operands)


def _step_of(count, limit=4):
    for k in range(limit, 0, -1):
        if count % k == 0:
            return k
    return 1

def _dot(a, b):
    return jnp.dot(a, b, precision=lax.Precision.HIGHEST)


def _inverse_factor(matrix, block):
    order = matrix.shape[0]
    nb = order // block
    eye = jnp.eye(block, dtype=matrix.dtype)
    rows = lax.broadcasted_iota(jnp.int32, (order, block), 0)
    identity = jnp.eye(order, dtype=matrix.dtype)

    def step(k, carry):
        trailing, lower, inverse = carry
        start = k * block
        head = lax.dynamic_slice(trailing, (start, start), (block, block))
        l_kk = jnp.linalg.cholesky(head)
        inv_kk = jax.scipy.linalg.solve_triangular(l_kk, eye, lower=True)
        l_row = lax.dynamic_slice(lower, (start, 0), (block, order))
        e_row = lax.dynamic_slice(identity, (start, 0), (block, order))
        inverse = lax.dynamic_update_slice(
            inverse, _dot(inv_kk, e_row - _dot(l_row, inverse)), (start, 0)
        )
        column = lax.dynamic_slice(trailing, (0, start), (order, block))
        below = jnp.where(rows >= start + block, _dot(column, inv_kk.T), jnp.zeros_like(column))
        lower = lax.dynamic_update_slice(lower, below, (0, start))
        trailing = trailing - _dot(below, below.T)
        return trailing, lower, inverse

    zeros = jnp.zeros_like(matrix)
    _, _, inverse = lax.fori_loop(0, nb, step, (matrix, zeros, zeros))
    return inverse

def on_device(diag_blocks, panel, local_targets, local_pairs, top_targets, top_pairs, top_pattern):
    diagonal = diag_blocks[0]
    order = diagonal.shape[0]
    rows_local = panel[0]
    count, width, depth = rows_local.shape
    inverse = _inverse_factor(diagonal, 128)
    flat = rows_local.reshape(count * width, depth)
    joined = jnp.dot(flat, inverse.T, precision=lax.Precision.HIGHEST)
    panel_here = joined.reshape(count, width, depth).astype(jnp.bfloat16)

    rows_all = lax.all_gather(panel_here, "blk", axis=0, tiled=True)

    def position(g):
        return g

    targets_here = local_targets[0]
    pairs_here = local_pairs[0]
    live = (pairs_here[:, 0] >= 0).astype(jnp.int32)
    left = position(jnp.maximum(pairs_here[:, 0], 0))
    right = position(jnp.maximum(pairs_here[:, 1], 0))
    slots = targets_here.shape[0]
    updated = pair_products(rows_all, left, right, live, targets_here, _step_of(slots))

    pattern = top_pattern[0]
    pairs_column = top_pairs[0]
    left_pos = jnp.take(pattern, pairs_column[:, 0], mode="clip")
    right_pos = jnp.take(pattern, pairs_column[:, 1], mode="clip")
    present = ((left_pos >= 0) & (right_pos >= 0)).astype(jnp.int32)
    top_count = pairs_column.shape[0]
    partial = pair_products(
        rows_all,
        position(jnp.maximum(left_pos, 0)),
        position(jnp.maximum(right_pos, 0)),
        present,
        None,
        _step_of(top_count),
    )
    summed = lax.psum_scatter(partial, "leaf", scatter_dimension=0, tiled=True).astype(jnp.float32)
    top_out = (top_targets[0].astype(jnp.float32) - summed).astype(jnp.bfloat16)[None]
    return (panel_here[None], updated[None], top_out)


def solution(mesh):
    in_specs = (
        P("leaf", None, None),
        P("leaf", "blk", None, None),
        P("leaf", "blk", None, None),
        P("leaf", "blk", None),
        P("blk", "leaf", None, None),
        P("blk", None, None),
        P("leaf", None),
    )
    out_specs = (
        P("leaf", "blk", None, None),
        P("leaf", "blk", None, None),
        P("blk", "leaf", None, None),
    )
    return jax.shard_map(on_device, mesh=mesh, in_specs=in_specs, out_specs=out_specs, check_vma=False)
```

```python
import functools

import jax
import jax.numpy as jnp
from jax import lax
from jax.experimental import pallas as pl
from jax.experimental.pallas import tpu as pltpu
from jax.sharding import PartitionSpec as P


def _pair_kernel(k, has_targets, left_ref, right_ref, live_ref, *refs):
    lrefs = refs[:k]
    rrefs = refs[k:2 * k]
    out_ref = refs[-1]
    step = pl.program_id(0)
    for j in range(k):
        live = live_ref[step * k + j] > 0

        def product(j=j):
            return lax.dot_general(
                lrefs[j][0], rrefs[j][0], (((1,), (1,)), ((), ())),
                preferred_element_type=jnp.float32,
            )

        if has_targets:
            t_ref = refs[2 * k]

            @pl.when(live)
            def _(j=j):
                out_ref[j] = (t_ref[j].astype(jnp.float32) - product()).astype(out_ref.dtype)

            @pl.when(jnp.logical_not(live))
            def _(j=j):
                out_ref[j] = t_ref[j]
        else:

            @pl.when(live)
            def _(j=j):
                out_ref[j] = product().astype(out_ref.dtype)

            @pl.when(jnp.logical_not(live))
            def _(j=j):
                out_ref[j] = jnp.zeros(out_ref.shape[1:], out_ref.dtype)


def pair_products(rows_all, left, right, live, targets, k):
    count = left.shape[0]
    _, width, depth = rows_all.shape
    steps = count // k

    def row_map(j, which):
        def index(i, l_ref, r_ref, v_ref):
            ref = l_ref if which == 0 else r_ref
            return (ref[i * k + j], 0, 0)

        return index

    in_specs = [pl.BlockSpec((1, width, depth), row_map(j, 0)) for j in range(k)]
    in_specs += [pl.BlockSpec((1, width, depth), row_map(j, 1)) for j in range(k)]
    operands = [rows_all] * (2 * k)
    block_map = lambda i, l_ref, r_ref, v_ref: (i, 0, 0)
    if targets is not None:
        in_specs.append(pl.BlockSpec((k, width, width), block_map))
        operands.append(targets)
    grid_spec = pltpu.PrefetchScalarGridSpec(
        num_scalar_prefetch=3,
        grid=(steps,),
        in_specs=in_specs,
        out_specs=pl.BlockSpec((k, width, width), block_map),
    )
    flops = 2 * count * width * width * depth
    bytes_accessed = count * (2 * width * depth * 2 + 2 * width * width * 2)
    return pl.pallas_call(
        functools.partial(_pair_kernel, k, targets is not None),
        grid_spec=grid_spec,
        out_shape=jax.ShapeDtypeStruct((count, width, width), jnp.bfloat16),
        compiler_params=pltpu.CompilerParams(dimension_semantics=("arbitrary",)),
        cost_estimate=pl.CostEstimate(flops=flops, bytes_accessed=bytes_accessed, transcendentals=0),
    )(left, right, live, *operands)


def _step_of(count, limit=4):
    for k in range(limit, 0, -1):
        if count % k == 0:
            return k
    return 1

def _dot(a, b):
    return jnp.dot(a, b, precision=lax.Precision.HIGHEST)


def _inverse_factor(matrix, block):
    order = matrix.shape[0]
    nb = order // block
    eye = jnp.eye(block, dtype=matrix.dtype)
    trailing = matrix
    factor = {}
    diag_inv = []
    for k in range(nb):
        head = trailing[:block, :block]
        l_kk = jnp.linalg.cholesky(head)
        inv_kk = jax.scipy.linalg.solve_triangular(l_kk, eye, lower=True)
        diag_inv.append(inv_kk)
        if k + 1 < nb:
            below = _dot(trailing[block:, :block], inv_kk.T)
            for i in range(k + 1, nb):
                factor[(i, k)] = below[(i - k - 1) * block:(i - k) * block]
            trailing = trailing[block:, block:] - _dot(below, below.T)

    def inverse_of(lo, hi):
        if hi - lo == 1:
            return diag_inv[lo]
        mid = (lo + hi) // 2
        upper = inverse_of(lo, mid)
        lower = inverse_of(mid, hi)
        coupling = jnp.concatenate(
            [jnp.concatenate([factor[(i, j)] for j in range(lo, mid)], axis=1) for i in range(mid, hi)],
            axis=0,
        )
        corner = -_dot(lower, _dot(coupling, upper))
        top = jnp.concatenate([upper, jnp.zeros((upper.shape[0], lower.shape[1]), upper.dtype)], axis=1)
        bottom = jnp.concatenate([corner, lower], axis=1)
        return jnp.concatenate([top, bottom], axis=0)

    return inverse_of(0, nb)


def on_device(diag_blocks, panel, local_targets, local_pairs, top_targets, top_pairs, top_pattern):
    diagonal = diag_blocks[0]
    order = diagonal.shape[0]
    rows_local = panel[0]
    count, width, depth = rows_local.shape
    inverse = _inverse_factor(diagonal, 128)
    flat = rows_local.reshape(count * width, depth)
    joined = jnp.dot(flat, inverse.T, precision=lax.Precision.HIGHEST)
    panel_here = joined.reshape(count, width, depth).astype(jnp.bfloat16)

    rows_all = lax.all_gather(panel_here, "blk", axis=0, tiled=True)

    def position(g):
        return g

    targets_here = local_targets[0]
    pairs_here = local_pairs[0]
    live = (pairs_here[:, 0] >= 0).astype(jnp.int32)
    left = position(jnp.maximum(pairs_here[:, 0], 0))
    right = position(jnp.maximum(pairs_here[:, 1], 0))
    slots = targets_here.shape[0]
    updated = pair_products(rows_all, left, right, live, targets_here, _step_of(slots, 8))

    pattern = top_pattern[0]
    pairs_column = top_pairs[0]
    left_pos = jnp.take(pattern, pairs_column[:, 0], mode="clip")
    right_pos = jnp.take(pattern, pairs_column[:, 1], mode="clip")
    present = ((left_pos >= 0) & (right_pos >= 0)).astype(jnp.int32)
    top_count = pairs_column.shape[0]
    partial = pair_products(
        rows_all,
        position(jnp.maximum(left_pos, 0)),
        position(jnp.maximum(right_pos, 0)),
        present,
        None,
        _step_of(top_count),
    )
    summed = lax.psum_scatter(partial, "leaf", scatter_dimension=0, tiled=True).astype(jnp.float32)
    top_out = (top_targets[0].astype(jnp.float32) - summed).astype(jnp.bfloat16)[None]
    return (panel_here[None], updated[None], top_out)


def solution(mesh):
    in_specs = (
        P("leaf", None, None),
        P("leaf", "blk", None, None),
        P("leaf", "blk", None, None),
        P("leaf", "blk", None),
        P("blk", "leaf", None, None),
        P("blk", None, None),
        P("leaf", None),
    )
    out_specs = (
        P("leaf", "blk", None, None),
        P("leaf", "blk", None, None),
        P("blk", "leaf", None, None),
    )
    return jax.shard_map(on_device, mesh=mesh, in_specs=in_specs, out_specs=out_specs, check_vma=False)
```

```python
import functools

import jax
import jax.numpy as jnp
from jax import lax
from jax.experimental import pallas as pl
from jax.experimental.pallas import tpu as pltpu
from jax.sharding import PartitionSpec as P


def _pair_kernel(k, has_targets, left_ref, right_ref, live_ref, *refs):
    lrefs = refs[:k]
    rrefs = refs[k:2 * k]
    out_ref = refs[-1]
    step = pl.program_id(0)
    for j in range(k):
        live = live_ref[step * k + j] > 0

        def product(j=j):
            return lax.dot_general(
                lrefs[j][0], rrefs[j][0], (((1,), (1,)), ((), ())),
                preferred_element_type=jnp.float32,
            )

        if has_targets:
            t_ref = refs[2 * k]

            @pl.when(live)
            def _(j=j):
                out_ref[j] = (t_ref[j].astype(jnp.float32) - product()).astype(out_ref.dtype)

            @pl.when(jnp.logical_not(live))
            def _(j=j):
                out_ref[j] = t_ref[j]
        else:

            @pl.when(live)
            def _(j=j):
                out_ref[j] = product().astype(out_ref.dtype)

            @pl.when(jnp.logical_not(live))
            def _(j=j):
                out_ref[j] = jnp.zeros(out_ref.shape[1:], out_ref.dtype)


def pair_products(rows_all, left, right, live, targets, k):
    count = left.shape[0]
    _, width, depth = rows_all.shape
    steps = count // k

    def row_map(j, which):
        def index(i, l_ref, r_ref, v_ref):
            ref = l_ref if which == 0 else r_ref
            return (ref[i * k + j], 0, 0)

        return index

    in_specs = [pl.BlockSpec((1, width, depth), row_map(j, 0)) for j in range(k)]
    in_specs += [pl.BlockSpec((1, width, depth), row_map(j, 1)) for j in range(k)]
    operands = [rows_all] * (2 * k)
    block_map = lambda i, l_ref, r_ref, v_ref: (i, 0, 0)
    if targets is not None:
        in_specs.append(pl.BlockSpec((k, width, width), block_map))
        operands.append(targets)
    grid_spec = pltpu.PrefetchScalarGridSpec(
        num_scalar_prefetch=3,
        grid=(steps,),
        in_specs=in_specs,
        out_specs=pl.BlockSpec((k, width, width), block_map),
    )
    flops = 2 * count * width * width * depth
    bytes_accessed = count * (2 * width * depth * 2 + 2 * width * width * 2)
    return pl.pallas_call(
        functools.partial(_pair_kernel, k, targets is not None),
        grid_spec=grid_spec,
        out_shape=jax.ShapeDtypeStruct((count, width, width), jnp.bfloat16),
        compiler_params=pltpu.CompilerParams(
            dimension_semantics=("arbitrary",), vmem_limit_bytes=48 * 1024 * 1024
        ),
        cost_estimate=pl.CostEstimate(flops=flops, bytes_accessed=bytes_accessed, transcendentals=0),
    )(left, right, live, *operands)


def _step_of(count, limit=4):
    for k in range(limit, 0, -1):
        if count % k == 0:
            return k
    return 1

def _dot(a, b):
    return jnp.dot(a, b, precision=lax.Precision.HIGHEST)


def _inverse_factor(matrix, block):
    order = matrix.shape[0]
    nb = order // block
    eye = jnp.eye(block, dtype=matrix.dtype)
    trailing = matrix
    factor = {}
    diag_inv = []
    for k in range(nb):
        head = trailing[:block, :block]
        l_kk = jnp.linalg.cholesky(head)
        inv_kk = jax.scipy.linalg.solve_triangular(l_kk, eye, lower=True)
        diag_inv.append(inv_kk)
        if k + 1 < nb:
            below = _dot(trailing[block:, :block], inv_kk.T)
            for i in range(k + 1, nb):
                factor[(i, k)] = below[(i - k - 1) * block:(i - k) * block]
            trailing = trailing[block:, block:] - _dot(below, below.T)

    def inverse_of(lo, hi):
        if hi - lo == 1:
            return diag_inv[lo]
        mid = (lo + hi) // 2
        upper = inverse_of(lo, mid)
        lower = inverse_of(mid, hi)
        coupling = jnp.concatenate(
            [jnp.concatenate([factor[(i, j)] for j in range(lo, mid)], axis=1) for i in range(mid, hi)],
            axis=0,
        )
        corner = -_dot(lower, _dot(coupling, upper))
        top = jnp.concatenate([upper, jnp.zeros((upper.shape[0], lower.shape[1]), upper.dtype)], axis=1)
        bottom = jnp.concatenate([corner, lower], axis=1)
        return jnp.concatenate([top, bottom], axis=0)

    return inverse_of(0, nb)


def on_device(diag_blocks, panel, local_targets, local_pairs, top_targets, top_pairs, top_pattern):
    diagonal = diag_blocks[0]
    order = diagonal.shape[0]
    rows_local = panel[0]
    count, width, depth = rows_local.shape
    inverse = _inverse_factor(diagonal, 128)
    flat = rows_local.reshape(count * width, depth)
    joined = jnp.dot(flat, inverse.T, precision=lax.Precision.HIGHEST)
    panel_here = joined.reshape(count, width, depth).astype(jnp.bfloat16)

    rows_all = lax.all_gather(panel_here, "blk", axis=0, tiled=True)

    def position(g):
        return g

    targets_here = local_targets[0]
    pairs_here = local_pairs[0]
    live = (pairs_here[:, 0] >= 0).astype(jnp.int32)
    left = position(jnp.maximum(pairs_here[:, 0], 0))
    right = position(jnp.maximum(pairs_here[:, 1], 0))
    slots = targets_here.shape[0]
    updated = pair_products(rows_all, left, right, live, targets_here, _step_of(slots, 16))

    pattern = top_pattern[0]
    pairs_column = top_pairs[0]
    left_pos = jnp.take(pattern, pairs_column[:, 0], mode="clip")
    right_pos = jnp.take(pattern, pairs_column[:, 1], mode="clip")
    present = ((left_pos >= 0) & (right_pos >= 0)).astype(jnp.int32)
    top_count = pairs_column.shape[0]
    partial = pair_products(
        rows_all,
        position(jnp.maximum(left_pos, 0)),
        position(jnp.maximum(right_pos, 0)),
        present,
        None,
        _step_of(top_count),
    )
    summed = lax.psum_scatter(partial, "leaf", scatter_dimension=0, tiled=True).astype(jnp.float32)
    top_out = (top_targets[0].astype(jnp.float32) - summed).astype(jnp.bfloat16)[None]
    return (panel_here[None], updated[None], top_out)


def solution(mesh):
    in_specs = (
        P("leaf", None, None),
        P("leaf", "blk", None, None),
        P("leaf", "blk", None, None),
        P("leaf", "blk", None),
        P("blk", "leaf", None, None),
        P("blk", None, None),
        P("leaf", None),
    )
    out_specs = (
        P("leaf", "blk", None, None),
        P("leaf", "blk", None, None),
        P("blk", "leaf", None, None),
    )
    return jax.shard_map(on_device, mesh=mesh, in_specs=in_specs, out_specs=out_specs, check_vma=False)
```

```python
import functools

import jax
import jax.numpy as jnp
from jax import lax
from jax.experimental import pallas as pl
from jax.experimental.pallas import tpu as pltpu
from jax.sharding import PartitionSpec as P


def _pair_kernel(k, has_targets, left_ref, right_ref, live_ref, *refs):
    lrefs = refs[:k]
    rrefs = refs[k:2 * k]
    out_ref = refs[-1]
    step = pl.program_id(0)
    for j in range(k):
        live = live_ref[step * k + j] > 0

        def product(j=j):
            return lax.dot_general(
                lrefs[j][0], rrefs[j][0], (((1,), (1,)), ((), ())),
                preferred_element_type=jnp.float32,
            )

        if has_targets:
            t_ref = refs[2 * k]

            @pl.when(live)
            def _(j=j):
                out_ref[j] = (t_ref[j].astype(jnp.float32) - product()).astype(out_ref.dtype)

            @pl.when(jnp.logical_not(live))
            def _(j=j):
                out_ref[j] = t_ref[j]
        else:

            @pl.when(live)
            def _(j=j):
                out_ref[j] = product().astype(out_ref.dtype)

            @pl.when(jnp.logical_not(live))
            def _(j=j):
                out_ref[j] = jnp.zeros(out_ref.shape[1:], out_ref.dtype)


def pair_products(rows_all, left, right, live, targets, k):
    count = left.shape[0]
    _, width, depth = rows_all.shape
    steps = count // k
    left = _held(left, live, k)
    right = _held(right, live, k)

    def row_map(j, which):
        def index(i, l_ref, r_ref, v_ref):
            ref = l_ref if which == 0 else r_ref
            return (ref[i * k + j], 0, 0)

        return index

    in_specs = [pl.BlockSpec((1, width, depth), row_map(j, 0)) for j in range(k)]
    in_specs += [pl.BlockSpec((1, width, depth), row_map(j, 1)) for j in range(k)]
    operands = [rows_all] * (2 * k)
    block_map = lambda i, l_ref, r_ref, v_ref: (i, 0, 0)
    if targets is not None:
        in_specs.append(pl.BlockSpec((k, width, width), block_map))
        operands.append(targets)
    grid_spec = pltpu.PrefetchScalarGridSpec(
        num_scalar_prefetch=3,
        grid=(steps,),
        in_specs=in_specs,
        out_specs=pl.BlockSpec((k, width, width), block_map),
    )
    flops = 2 * count * width * width * depth
    bytes_accessed = count * (2 * width * depth * 2 + 2 * width * width * 2)
    return pl.pallas_call(
        functools.partial(_pair_kernel, k, targets is not None),
        grid_spec=grid_spec,
        out_shape=jax.ShapeDtypeStruct((count, width, width), jnp.bfloat16),
        compiler_params=pltpu.CompilerParams(dimension_semantics=("arbitrary",)),
        cost_estimate=pl.CostEstimate(flops=flops, bytes_accessed=bytes_accessed, transcendentals=0),
    )(left, right, live, *operands)


def _held(index, live, k):
    index = index.reshape(-1, k)
    keep = live.reshape(-1, k) > 0
    rows = [index[0]]
    for i in range(1, index.shape[0]):
        rows.append(jnp.where(keep[i], index[i], rows[-1]))
    return jnp.stack(rows).reshape(-1)


def _step_of(count, limit=4):
    for k in range(limit, 0, -1):
        if count % k == 0:
            return k
    return 1

def _dot(a, b):
    return jnp.dot(a, b, precision=lax.Precision.HIGHEST)


def _inverse_factor(matrix, block):
    order = matrix.shape[0]
    nb = order // block
    eye = jnp.eye(block, dtype=matrix.dtype)
    trailing = matrix
    factor = {}
    diag_inv = []
    for k in range(nb):
        head = trailing[:block, :block]
        l_kk = jnp.linalg.cholesky(head)
        inv_kk = jax.scipy.linalg.solve_triangular(l_kk, eye, lower=True)
        diag_inv.append(inv_kk)
        if k + 1 < nb:
            below = _dot(trailing[block:, :block], inv_kk.T)
            for i in range(k + 1, nb):
                factor[(i, k)] = below[(i - k - 1) * block:(i - k) * block]
            trailing = trailing[block:, block:] - _dot(below, below.T)

    def inverse_of(lo, hi):
        if hi - lo == 1:
            return diag_inv[lo]
        mid = (lo + hi) // 2
        upper = inverse_of(lo, mid)
        lower = inverse_of(mid, hi)
        coupling = jnp.concatenate(
            [jnp.concatenate([factor[(i, j)] for j in range(lo, mid)], axis=1) for i in range(mid, hi)],
            axis=0,
        )
        corner = -_dot(lower, _dot(coupling, upper))
        top = jnp.concatenate([upper, jnp.zeros((upper.shape[0], lower.shape[1]), upper.dtype)], axis=1)
        bottom = jnp.concatenate([corner, lower], axis=1)
        return jnp.concatenate([top, bottom], axis=0)

    return inverse_of(0, nb)


def on_device(diag_blocks, panel, local_targets, local_pairs, top_targets, top_pairs, top_pattern):
    diagonal = diag_blocks[0]
    order = diagonal.shape[0]
    rows_local = panel[0]
    count, width, depth = rows_local.shape
    inverse = _inverse_factor(diagonal, 128)
    flat = rows_local.reshape(count * width, depth)
    joined = jnp.dot(flat, inverse.T, precision=lax.Precision.HIGHEST)
    panel_here = joined.reshape(count, width, depth).astype(jnp.bfloat16)

    rows_all = lax.all_gather(panel_here, "blk", axis=0, tiled=True)

    def position(g):
        return g

    targets_here = local_targets[0]
    pairs_here = local_pairs[0]
    live = (pairs_here[:, 0] >= 0).astype(jnp.int32)
    left = position(jnp.maximum(pairs_here[:, 0], 0))
    right = position(jnp.maximum(pairs_here[:, 1], 0))
    slots = targets_here.shape[0]
    updated = pair_products(rows_all, left, right, live, targets_here, _step_of(slots, 8))

    pattern = top_pattern[0]
    pairs_column = top_pairs[0]
    left_pos = jnp.take(pattern, pairs_column[:, 0], mode="clip")
    right_pos = jnp.take(pattern, pairs_column[:, 1], mode="clip")
    present = ((left_pos >= 0) & (right_pos >= 0)).astype(jnp.int32)
    top_count = pairs_column.shape[0]
    partial = pair_products(
        rows_all,
        position(jnp.maximum(left_pos, 0)),
        position(jnp.maximum(right_pos, 0)),
        present,
        None,
        _step_of(top_count),
    )
    summed = lax.psum_scatter(partial, "leaf", scatter_dimension=0, tiled=True).astype(jnp.float32)
    top_out = (top_targets[0].astype(jnp.float32) - summed).astype(jnp.bfloat16)[None]
    return (panel_here[None], updated[None], top_out)


def solution(mesh):
    in_specs = (
        P("leaf", None, None),
        P("leaf", "blk", None, None),
        P("leaf", "blk", None, None),
        P("leaf", "blk", None),
        P("blk", "leaf", None, None),
        P("blk", None, None),
        P("leaf", None),
    )
    out_specs = (
        P("leaf", "blk", None, None),
        P("leaf", "blk", None, None),
        P("blk", "leaf", None, None),
    )
    return jax.shard_map(on_device, mesh=mesh, in_specs=in_specs, out_specs=out_specs, check_vma=False)
```

```python
import functools

import jax
import jax.numpy as jnp
from jax import lax
from jax.experimental import pallas as pl
from jax.experimental.pallas import tpu as pltpu
from jax.sharding import PartitionSpec as P


def _pair_kernel(k, has_targets, left_ref, right_ref, live_ref, *refs):
    lrefs = refs[:k]
    rrefs = refs[k:2 * k]
    out_ref = refs[-1]
    step = pl.program_id(0)
    for j in range(k):
        live = live_ref[step * k + j] > 0

        def product(j=j):
            return lax.dot_general(
                lrefs[j][0], rrefs[j][0], (((1,), (1,)), ((), ())),
                preferred_element_type=jnp.float32,
            )

        if has_targets:
            t_ref = refs[2 * k]

            @pl.when(live)
            def _(j=j):
                out_ref[j] = (t_ref[j].astype(jnp.float32) - product()).astype(out_ref.dtype)

            @pl.when(jnp.logical_not(live))
            def _(j=j):
                out_ref[j] = t_ref[j]
        else:

            @pl.when(live)
            def _(j=j):
                out_ref[j] = product().astype(out_ref.dtype)

            @pl.when(jnp.logical_not(live))
            def _(j=j):
                out_ref[j] = jnp.zeros(out_ref.shape[1:], out_ref.dtype)


def pair_products(rows_all, left, right, live, targets, k):
    count = left.shape[0]
    _, width, depth = rows_all.shape
    steps = count // k
    left = _held(left, live, k)
    right = _held(right, live, k)

    def row_map(j, which):
        def index(i, l_ref, r_ref, v_ref):
            ref = l_ref if which == 0 else r_ref
            return (ref[i * k + j], 0, 0)

        return index

    in_specs = [pl.BlockSpec((1, width, depth), row_map(j, 0)) for j in range(k)]
    in_specs += [pl.BlockSpec((1, width, depth), row_map(j, 1)) for j in range(k)]
    operands = [rows_all] * (2 * k)
    block_map = lambda i, l_ref, r_ref, v_ref: (i, 0, 0)
    if targets is not None:
        in_specs.append(pl.BlockSpec((k, width, width), block_map))
        operands.append(targets)
    grid_spec = pltpu.PrefetchScalarGridSpec(
        num_scalar_prefetch=3,
        grid=(steps,),
        in_specs=in_specs,
        out_specs=pl.BlockSpec((k, width, width), block_map),
    )
    flops = 2 * count * width * width * depth
    bytes_accessed = count * (2 * width * depth * 2 + 2 * width * width * 2)
    return pl.pallas_call(
        functools.partial(_pair_kernel, k, targets is not None),
        grid_spec=grid_spec,
        out_shape=jax.ShapeDtypeStruct((count, width, width), jnp.bfloat16),
        compiler_params=pltpu.CompilerParams(dimension_semantics=("arbitrary",)),
        cost_estimate=pl.CostEstimate(flops=flops, bytes_accessed=bytes_accessed, transcendentals=0),
    )(left, right, live, *operands)


def _held(index, live, k):
    index = index.reshape(-1, k)
    keep = live.reshape(-1, k) > 0
    rows = [index[0]]
    for i in range(1, index.shape[0]):
        rows.append(jnp.where(keep[i], index[i], rows[-1]))
    return jnp.stack(rows).reshape(-1)


def _step_of(count, limit=4):
    for k in range(limit, 0, -1):
        if count % k == 0:
            return k
    return 1

def _dot(a, b):
    return jnp.dot(a, b, precision=lax.Precision.HIGHEST)


def _inverse_factor(matrix, block):
    order = matrix.shape[0]
    nb = order // block
    eye = jnp.eye(block, dtype=matrix.dtype)
    trailing = matrix
    factor = {}
    diag_inv = []
    for k in range(nb):
        head = trailing[:block, :block]
        l_kk = jnp.linalg.cholesky(head)
        inv_kk = jax.scipy.linalg.solve_triangular(l_kk, eye, lower=True)
        diag_inv.append(inv_kk)
        if k + 1 < nb:
            below = _dot(trailing[block:, :block], inv_kk.T)
            for i in range(k + 1, nb):
                factor[(i, k)] = below[(i - k - 1) * block:(i - k) * block]
            trailing = trailing[block:, block:] - _dot(below, below.T)

    def inverse_of(lo, hi):
        if hi - lo == 1:
            return diag_inv[lo]
        mid = (lo + hi) // 2
        upper = inverse_of(lo, mid)
        lower = inverse_of(mid, hi)
        coupling = jnp.concatenate(
            [jnp.concatenate([factor[(i, j)] for j in range(lo, mid)], axis=1) for i in range(mid, hi)],
            axis=0,
        )
        corner = -_dot(lower, _dot(coupling, upper))
        top = jnp.concatenate([upper, jnp.zeros((upper.shape[0], lower.shape[1]), upper.dtype)], axis=1)
        bottom = jnp.concatenate([corner, lower], axis=1)
        return jnp.concatenate([top, bottom], axis=0)

    return inverse_of(0, nb)


def on_device(diag_blocks, panel, local_targets, local_pairs, top_targets, top_pairs, top_pattern):
    diagonal = diag_blocks[0]
    order = diagonal.shape[0]
    rows_local = panel[0]
    count, width, depth = rows_local.shape
    inverse = _inverse_factor(diagonal, 128)
    flat = rows_local.reshape(count * width, depth)
    joined = jnp.dot(flat, inverse.T, precision=lax.Precision.HIGHEST)
    panel_here = joined.reshape(count, width, depth).astype(jnp.bfloat16)

    rows_all = lax.all_gather(panel_here, "blk", axis=0, tiled=True)

    def position(g):
        return g

    targets_here = local_targets[0]
    pairs_here = local_pairs[0]
    live = (pairs_here[:, 0] >= 0).astype(jnp.int32)
    left = position(jnp.maximum(pairs_here[:, 0], 0))
    right = position(jnp.maximum(pairs_here[:, 1], 0))
    slots = targets_here.shape[0]
    updated = pair_products(rows_all, left, right, live, targets_here, _step_of(slots, 8))

    pattern = top_pattern[0]
    pairs_column = top_pairs[0]
    left_pos = jnp.take(pattern, pairs_column[:, 0], mode="clip")
    right_pos = jnp.take(pattern, pairs_column[:, 1], mode="clip")
    present = ((left_pos >= 0) & (right_pos >= 0)).astype(jnp.int32)
    top_count = pairs_column.shape[0]
    partial = pair_products(
        rows_all,
        position(jnp.maximum(left_pos, 0)),
        position(jnp.maximum(right_pos, 0)),
        present,
        None,
        _step_of(top_count, 8),
    )
    summed = lax.psum_scatter(partial, "leaf", scatter_dimension=0, tiled=True).astype(jnp.float32)
    top_out = (top_targets[0].astype(jnp.float32) - summed).astype(jnp.bfloat16)[None]
    return (panel_here[None], updated[None], top_out)


def solution(mesh):
    in_specs = (
        P("leaf", None, None),
        P("leaf", "blk", None, None),
        P("leaf", "blk", None, None),
        P("leaf", "blk", None),
        P("blk", "leaf", None, None),
        P("blk", None, None),
        P("leaf", None),
    )
    out_specs = (
        P("leaf", "blk", None, None),
        P("leaf", "blk", None, None),
        P("blk", "leaf", None, None),
    )
    return jax.shard_map(on_device, mesh=mesh, in_specs=in_specs, out_specs=out_specs, check_vma=False)
```

```python
import functools

import jax
import jax.numpy as jnp
from jax import lax
from jax.experimental import pallas as pl
from jax.experimental.pallas import tpu as pltpu
from jax.sharding import PartitionSpec as P


def _pair_kernel(k, has_targets, left_ref, right_ref, live_ref, *refs):
    lrefs = refs[:k]
    rrefs = refs[k:2 * k]
    out_ref = refs[-1]
    step = pl.program_id(0)
    for j in range(k):
        live = live_ref[step * k + j] > 0

        def product(j=j):
            return lax.dot_general(
                lrefs[j][0], rrefs[j][0], (((1,), (1,)), ((), ())),
                preferred_element_type=jnp.float32,
            )

        if has_targets:
            t_ref = refs[2 * k]

            @pl.when(live)
            def _(j=j):
                out_ref[j] = (t_ref[j].astype(jnp.float32) - product()).astype(out_ref.dtype)

            @pl.when(jnp.logical_not(live))
            def _(j=j):
                out_ref[j] = t_ref[j]
        else:

            @pl.when(live)
            def _(j=j):
                out_ref[j] = product().astype(out_ref.dtype)

            @pl.when(jnp.logical_not(live))
            def _(j=j):
                out_ref[j] = jnp.zeros(out_ref.shape[1:], out_ref.dtype)


def pair_products(rows_all, left, right, live, targets, k):
    count = left.shape[0]
    _, width, depth = rows_all.shape
    steps = count // k
    left = _held(left, live, k)
    right = _held(right, live, k)

    def row_map(j, which):
        def index(i, l_ref, r_ref, v_ref):
            ref = l_ref if which == 0 else r_ref
            return (ref[i * k + j], 0, 0)

        return index

    in_specs = [pl.BlockSpec((1, width, depth), row_map(j, 0)) for j in range(k)]
    in_specs += [pl.BlockSpec((1, width, depth), row_map(j, 1)) for j in range(k)]
    operands = [rows_all] * (2 * k)
    block_map = lambda i, l_ref, r_ref, v_ref: (i, 0, 0)
    if targets is not None:
        in_specs.append(pl.BlockSpec((k, width, width), block_map))
        operands.append(targets)
    grid_spec = pltpu.PrefetchScalarGridSpec(
        num_scalar_prefetch=3,
        grid=(steps,),
        in_specs=in_specs,
        out_specs=pl.BlockSpec((k, width, width), block_map),
    )
    flops = 2 * count * width * width * depth
    bytes_accessed = count * (2 * width * depth * 2 + 2 * width * width * 2)
    return pl.pallas_call(
        functools.partial(_pair_kernel, k, targets is not None),
        grid_spec=grid_spec,
        out_shape=jax.ShapeDtypeStruct((count, width, width), jnp.bfloat16),
        compiler_params=pltpu.CompilerParams(dimension_semantics=("arbitrary",)),
        cost_estimate=pl.CostEstimate(flops=flops, bytes_accessed=bytes_accessed, transcendentals=0),
    )(left, right, live, *operands)


def _held(index, live, k):
    index = index.reshape(-1, k)
    keep = live.reshape(-1, k) > 0
    rows = [index[0]]
    for i in range(1, index.shape[0]):
        rows.append(jnp.where(keep[i], index[i], rows[-1]))
    return jnp.stack(rows).reshape(-1)


def _step_of(count, limit=4):
    for k in range(limit, 0, -1):
        if count % k == 0:
            return k
    return 1

def _dot(a, b):
    return jnp.dot(a, b, precision=lax.Precision.HIGHEST)


def _inverse_factor(matrix, block):
    order = matrix.shape[0]
    nb = order // block
    eye = jnp.eye(block, dtype=matrix.dtype)
    trailing = matrix
    factor = {}
    diag_inv = []
    for k in range(nb):
        head = trailing[:block, :block]
        l_kk = jnp.linalg.cholesky(head)
        inv_kk = jax.scipy.linalg.solve_triangular(l_kk, eye, lower=True)
        diag_inv.append(inv_kk)
        if k + 1 < nb:
            below = _dot(trailing[block:, :block], inv_kk.T)
            for i in range(k + 1, nb):
                factor[(i, k)] = below[(i - k - 1) * block:(i - k) * block]
            trailing = trailing[block:, block:] - _dot(below, below.T)

    def inverse_of(lo, hi):
        if hi - lo == 1:
            return diag_inv[lo]
        mid = (lo + hi) // 2
        upper = inverse_of(lo, mid)
        lower = inverse_of(mid, hi)
        coupling = jnp.concatenate(
            [jnp.concatenate([factor[(i, j)] for j in range(lo, mid)], axis=1) for i in range(mid, hi)],
            axis=0,
        )
        corner = -_dot(lower, _dot(coupling, upper))
        top = jnp.concatenate([upper, jnp.zeros((upper.shape[0], lower.shape[1]), upper.dtype)], axis=1)
        bottom = jnp.concatenate([corner, lower], axis=1)
        return jnp.concatenate([top, bottom], axis=0)

    return inverse_of(0, nb)


def on_device(diag_blocks, panel, local_targets, local_pairs, top_targets, top_pairs, top_pattern):
    diagonal = diag_blocks[0]
    order = diagonal.shape[0]
    rows_local = panel[0]
    count, width, depth = rows_local.shape
    inverse = _inverse_factor(diagonal, 128)
    flat = rows_local.reshape(count * width, depth)
    joined = jnp.dot(flat, inverse.T, precision=lax.Precision.HIGH)
    panel_here = joined.reshape(count, width, depth).astype(jnp.bfloat16)

    rows_all = lax.all_gather(panel_here, "blk", axis=0, tiled=True)

    def position(g):
        return g

    targets_here = local_targets[0]
    pairs_here = local_pairs[0]
    live = (pairs_here[:, 0] >= 0).astype(jnp.int32)
    left = position(jnp.maximum(pairs_here[:, 0], 0))
    right = position(jnp.maximum(pairs_here[:, 1], 0))
    slots = targets_here.shape[0]
    updated = pair_products(rows_all, left, right, live, targets_here, _step_of(slots, 8))

    pattern = top_pattern[0]
    pairs_column = top_pairs[0]
    left_pos = jnp.take(pattern, pairs_column[:, 0], mode="clip")
    right_pos = jnp.take(pattern, pairs_column[:, 1], mode="clip")
    present = ((left_pos >= 0) & (right_pos >= 0)).astype(jnp.int32)
    top_count = pairs_column.shape[0]
    partial = pair_products(
        rows_all,
        position(jnp.maximum(left_pos, 0)),
        position(jnp.maximum(right_pos, 0)),
        present,
        None,
        _step_of(top_count),
    )
    summed = lax.psum_scatter(partial, "leaf", scatter_dimension=0, tiled=True).astype(jnp.float32)
    top_out = (top_targets[0].astype(jnp.float32) - summed).astype(jnp.bfloat16)[None]
    return (panel_here[None], updated[None], top_out)


def solution(mesh):
    in_specs = (
        P("leaf", None, None),
        P("leaf", "blk", None, None),
        P("leaf", "blk", None, None),
        P("leaf", "blk", None),
        P("blk", "leaf", None, None),
        P("blk", None, None),
        P("leaf", None),
    )
    out_specs = (
        P("leaf", "blk", None, None),
        P("leaf", "blk", None, None),
        P("blk", "leaf", None, None),
    )
    return jax.shard_map(on_device, mesh=mesh, in_specs=in_specs, out_specs=out_specs, check_vma=False)
```
